256 devices in a mesh: dom: 16 (over x, y), slab: 16 (over z, core).
Axes of the slice: x: 4, y: 4, z: 8, core: 2. Of those that a mesh axis runs over, the one named last changes fastest.
Arguments:
- images: bfloat16 [4096, 8192], P(('dom', 'slab')), may hold values from -64 to 64
- defocus: bfloat16 [4096], P(('dom', 'slab')), may hold values from 20 to 60
- inv_noise: float32 [4096], replicated, may hold values from 0.01 to 0.04
- slices: bfloat16 [128, 8192], P('slab'), may hold values from -5 to 5
- lists: int32 [4096, 32], P(('dom', 'slab')), may hold values from 0 to 127, as said below
- counts: int32 [4096], P(('dom', 'slab')), may hold values from 0 to 32, as said below
Outputs:
- peak_weight: float32 [4096], P(('dom', 'slab'))
- data_sum: float32 [128, 8192], P('slab', 'dom')
- weight_sum: float32 [128, 4096], P('slab', 'dom')
The draws below stay inside these ranges and needn't reach their ends.
Inputs may be any that keep to these rules, and one draw needn't show every extreme that they name: `lists`: the 32 entries of a row are different orientations. `counts`: 0 marks a particle left out of this pass; a particle that takes part has 2 or more significant orientations.
All inputs are finite; a program needn't handle non-finite values.
Results may differ from the reference program's by a relative error of at most 0.009.
Values may be sent and summed in bfloat16 or wider, within the bound.
No kernel may reach another device: no remote copies, remote signals or barrier semaphores. Data moves between devices by JAX's collectives and lax.ppermute only.
A program may use at most 128 MiB of HBM per device.

```python
import math
import jax
import jax.numpy as jnp
from jax import lax

SIDE = 64
COEF = 4096
PIX = 8192
TRANS = 25
LMAX = 32
ORIENT = 128
PARTICLES = 4096
GROUP = 256


def defocus_values(key):
    return jax.random.uniform(jax.random.fold_in(key, 11), (PARTICLES,), jnp.float32, 20.0, 60.0)


def slice_values(key):
    return jnp.clip(jax.random.normal(jax.random.fold_in(key, 12), (ORIENT, PIX), jnp.float32), -5.0, 5.0)


def list_values(key):
    center = jax.random.randint(jax.random.fold_in(key, 13), (PARTICLES,), 0, ORIENT, dtype=jnp.int32)
    stride = jax.random.randint(jax.random.fold_in(key, 14), (PARTICLES,), 1, ORIENT // LMAX + 1, dtype=jnp.int32)
    slots = jnp.arange(LMAX, dtype=jnp.int32)
    return ((center[:, None] + slots[None, :] * stride[:, None]) % ORIENT).astype(jnp.int32)


def draw_defocus(key, part):
    return defocus_values(key).astype(jnp.bfloat16)


def draw_slices(key, part):
    return slice_values(key).astype(jnp.bfloat16)


def draw_lists(key, part):
    return list_values(key)


def draw_counts(key, part):
    particle = jnp.arange(PARTICLES, dtype=jnp.int32)
    band = particle // GROUP % 4
    chance = jax.random.randint(jax.random.fold_in(key, 15), (PARTICLES,), 0, 8, dtype=jnp.int32)
    alive = chance < jnp.left_shift(jnp.int32(1), 3 - band)
    length = jax.random.randint(jax.random.fold_in(key, 16), (PARTICLES,), 2, LMAX + 1, dtype=jnp.int32)
    result = jnp.where(alive, length, 0).astype(jnp.int32)
    return result.at[0].set(LMAX).at[1].set(0)


def draw_images(key, part):
    values = jax.random.normal(jax.random.fold_in(key, 17), (PARTICLES, PIX), jnp.float32)
    return jnp.clip(values, -64.0, 64.0).astype(jnp.bfloat16)


def setup_inputs(seed: int = 0) -> dict:
    seeds = jax.random.split(jax.random.key(seed), 7)
    return {
        "images": draw_images(jax.random.fold_in(seeds[6], 71), 0),
        "defocus": draw_defocus(jax.random.fold_in(seeds[6], 71), 0),
        "inv_noise": jnp.clip(jnp.exp(jax.random.uniform(seeds[2], (COEF,), jnp.float32, math.log(0.01), math.log(0.04))), 0.01, 0.04),
        "slices": draw_slices(jax.random.fold_in(seeds[6], 71), 0),
        "lists": draw_lists(jax.random.fold_in(seeds[6], 71), 0),
        "counts": draw_counts(jax.random.fold_in(seeds[6], 71), 0),
    }


SENTINEL = -1e+30
HIGHEST = lax.Precision.HIGHEST

def round_half(values):
    return lax.optimization_barrier(values.astype(jnp.bfloat16)).astype(jnp.float32)

def frequency_grid():
    position = jnp.arange(COEF, dtype=jnp.int32)
    freq_x = (position // SIDE - SIDE // 2).astype(jnp.float32)
    freq_y = (position % SIDE - SIDE // 2).astype(jnp.float32)
    return (freq_x, freq_y)

def shift_tables(freq_x, freq_y):
    edge = math.isqrt(TRANS)
    half = edge // 2
    offsets = jnp.arange(TRANS, dtype=jnp.int32)
    shift_x = (offsets // edge - half).astype(jnp.float32)
    shift_y = (offsets % edge - half).astype(jnp.float32)
    angle = 2.0 * jnp.pi * (shift_x[:, None] * freq_x[None, :] + shift_y[:, None] * freq_y[None, :]) / SIDE
    return (jnp.cos(angle), jnp.sin(angle))

def transfer_function(defocus, freq_x, freq_y):
    radius = (freq_x * freq_x + freq_y * freq_y) / (SIDE * SIDE)
    return -jnp.sin(jnp.pi * defocus.astype(jnp.float32)[:, None] * radius[None, :] + 0.1)

def rotate_rows(values, cosine, sine):
    real_part = values[:, None, :COEF]
    imag_part = values[:, None, COEF:]
    turned = jnp.concatenate((real_part * cosine - imag_part * sine, real_part * sine + imag_part * cosine), axis=-1)
    return turned.reshape(values.shape[0] * TRANS, 2 * COEF)

def significance(lists, counts, offset, number):
    orient_ids = offset + jnp.arange(number, dtype=jnp.int32)
    slot_live = jnp.arange(lists.shape[1], dtype=jnp.int32)[None, :] < counts[:, None]
    hits = (lists[:, :, None] == orient_ids[None, None, :]) & slot_live[:, :, None]
    return jnp.any(hits, axis=1)

def reference(images, defocus, inv_noise, slices, lists, counts):
    freq_x, freq_y = frequency_grid()
    cosine, sine = shift_tables(freq_x, freq_y)
    slices_wide = slices.astype(jnp.float32)
    squares = round_half(slices_wide * slices_wide)
    block = 128

    def one_block(sums, block_index):
        start = (block_index * block).astype(jnp.int32)
        part_images = lax.dynamic_slice_in_dim(images, start, block, 0)
        part_defocus = lax.dynamic_slice_in_dim(defocus, start, block, 0)
        part_lists = lax.dynamic_slice_in_dim(lists, start, block, 0)
        part_counts = lax.dynamic_slice_in_dim(counts, start, block, 0)
        ctf = transfer_function(part_defocus, freq_x, freq_y)
        real_part = part_images[:, :COEF].astype(jnp.float32)
        imag_part = part_images[:, COEF:].astype(jnp.float32)
        weighted = round_half(jnp.concatenate((inv_noise * ctf * real_part, inv_noise * ctf * imag_part), axis=-1))
        image_half = round_half(jnp.concatenate((ctf * real_part, ctf * imag_part), axis=-1))
        quad_half = -0.5 * inv_noise * ctf * ctf
        quadratic = round_half(jnp.concatenate((quad_half, quad_half), axis=-1))
        linear = lax.dot_general(rotate_rows(weighted, cosine, sine), slices_wide, (((1,), (1,)), ((), ())), precision=HIGHEST).reshape(block, TRANS, ORIENT)
        energy = lax.dot_general(quadratic, squares, (((1,), (1,)), ((), ())), precision=HIGHEST)
        score = linear + energy[:, None, :]
        mask = significance(part_lists, part_counts, 0, ORIENT)
        score = jnp.where(mask[:, None, :], score, SENTINEL)
        alive = part_counts > 0
        highest = jnp.where(alive, lax.optimization_barrier(jnp.max(score, axis=(1, 2))), 0.0)
        expo = jnp.where(mask[:, None, :], jnp.exp(score - highest[:, None, None]), 0.0)
        normalizer = jnp.where(alive, lax.optimization_barrier(jnp.sum(expo, axis=(1, 2))), 1.0)
        posterior = round_half(expo / normalizer[:, None, None])
        peak_part = jnp.where(alive, 1.0 / normalizer, 0.0)
        data = sums[0] + lax.dot_general(posterior.reshape(block * TRANS, ORIENT), rotate_rows(image_half, cosine, sine), (((0,), (0,)), ((), ())), precision=HIGHEST)
        ctf_half = round_half(ctf * ctf)
        weight = sums[1] + lax.dot_general(lax.optimization_barrier(jnp.sum(posterior, axis=1)), ctf_half, (((0,), (0,)), ((), ())), precision=HIGHEST)
        return ((data, weight), peak_part)
    start_sums = (jnp.zeros((ORIENT, PIX), jnp.float32), jnp.zeros((ORIENT, COEF), jnp.float32))
    (data_sum, weight_sum), peaks = lax.scan(one_block, start_sums, jnp.arange(PARTICLES // block, dtype=jnp.int32))
    return (peaks.reshape(PARTICLES), data_sum, weight_sum)
```

```python
import math

import numpy as np
import jax
import jax.numpy as jnp
from jax import lax
from jax.sharding import Mesh
from jax.sharding import PartitionSpec as P

SIDE = 64
COEF = 4096
PIX = 2 * COEF
TRANS = 25

SENTINEL = -1e30
HIGHEST = lax.Precision.HIGHEST


def _tables():
    position = np.arange(COEF)
    freq_x = (position // SIDE - SIDE // 2).astype(np.float64)
    freq_y = (position % SIDE - SIDE // 2).astype(np.float64)
    edge = math.isqrt(TRANS)
    half = edge // 2
    offsets = np.arange(TRANS)
    shift_x = (offsets // edge - half).astype(np.float64)
    shift_y = (offsets % edge - half).astype(np.float64)
    angle = 2.0 * np.pi * (shift_x[:, None] * freq_x[None, :] + shift_y[:, None] * freq_y[None, :]) / SIDE
    radius = (freq_x * freq_x + freq_y * freq_y) / (SIDE * SIDE)
    return (
        np.cos(angle).astype(np.float32),
        np.sin(angle).astype(np.float32),
        radius.astype(np.float32),
    )


COSINE, SINE, RADIUS = _tables()


def split3(values):
    first = values.astype(jnp.bfloat16)
    rest = values - first.astype(jnp.float32)
    second = rest.astype(jnp.bfloat16)
    third = (rest - second.astype(jnp.float32)).astype(jnp.bfloat16)
    return first, second, third


def shards(images, defocus, inv_noise, slices, lists, counts):
    rows = images.shape[0]
    own_orients = slices.shape[0]
    orient_total = own_orients * lax.axis_size("zz") * lax.axis_size("cc")
    pad = (-(orient_total + 2)) % 128
    zz = lax.axis_index("zz")
    cc = lax.axis_index("cc")
    group = lax.axis_size("zz")

    orient_ids = jnp.arange(orient_total, dtype=jnp.int32)
    slot_live = jnp.arange(lists.shape[1], dtype=jnp.int32)[None, :] < counts[:, None]
    hits = (lists[:, :, None] == orient_ids[None, None, :]) & slot_live[:, :, None]
    mask_all = jnp.any(hits, axis=1)
    alive = counts > 0
    extra = jnp.concatenate(
        (
            mask_all.astype(jnp.bfloat16),
            alive.astype(jnp.bfloat16)[:, None],
            defocus[:, None],
            jnp.zeros((rows, pad), jnp.bfloat16),
        ),
        axis=1,
    )
    packed = jnp.concatenate((images, extra), axis=1)
    gathered = lax.all_gather(packed, "zz", axis=0, tiled=True)
    local_slices = lax.all_gather(slices, "cc", axis=0, tiled=True)
    count = gathered.shape[0]
    chip_orients = local_slices.shape[0]

    g_images = gathered[:, :PIX]
    g_mask_all = gathered[:, PIX : PIX + orient_total]
    g_alive = gathered[:, PIX + orient_total] > 0.5
    g_defocus = gathered[:, PIX + orient_total + 1].astype(jnp.float32)
    mask = lax.dynamic_slice_in_dim(g_mask_all, zz * chip_orients, chip_orients, 1) > 0.5

    cosine = jnp.asarray(COSINE)
    sine = jnp.asarray(SINE)
    radius = jnp.asarray(RADIUS)
    ctf = -jnp.sin(jnp.pi * g_defocus[:, None] * radius[None, :] + 0.1)
    real_part = g_images[:, :COEF].astype(jnp.float32)
    imag_part = g_images[:, COEF:].astype(jnp.float32)
    weighted = jnp.concatenate(
        (inv_noise * ctf * real_part, inv_noise * ctf * imag_part), axis=-1
    ).astype(jnp.bfloat16)
    image_half = jnp.concatenate((ctf * real_part, ctf * imag_part), axis=-1).astype(jnp.bfloat16)
    quad_half = (-0.5 * inv_noise * ctf * ctf).astype(jnp.bfloat16)
    ctf_half = (ctf * ctf).astype(jnp.bfloat16)

    slices_wide = local_slices.astype(jnp.float32)
    squares = (slices_wide * slices_wide).astype(jnp.bfloat16)
    energy = lax.dot_general(
        quad_half, squares[:, :COEF], (((1,), (1,)), ((), ())), preferred_element_type=jnp.float32
    ) + lax.dot_general(
        quad_half, squares[:, COEF:], (((1,), (1,)), ((), ())), preferred_element_type=jnp.float32
    )

    s_real = slices_wide[None, :, :COEF]
    s_imag = slices_wide[None, :, COEF:]
    c_t = cosine[:, None, :]
    s_t = sine[:, None, :]
    turned = jnp.concatenate((c_t * s_real + s_t * s_imag, c_t * s_imag - s_t * s_real), axis=-1)
    turned = turned.reshape(TRANS * chip_orients, PIX)
    parts = jnp.concatenate(split3(turned), axis=0)
    linear3 = lax.dot_general(
        weighted, parts, (((1,), (1,)), ((), ())), preferred_element_type=jnp.float32
    )
    block = TRANS * chip_orients
    linear = linear3[:, :block] + linear3[:, block : 2 * block] + linear3[:, 2 * block :]
    linear = linear.reshape(count, TRANS, chip_orients)
    score = jnp.where(mask[:, None, :], linear + energy[:, None, :], SENTINEL)

    local_max = jnp.max(score, axis=(1, 2))
    local_sum = jnp.sum(
        jnp.where(mask[:, None, :], jnp.exp(score - local_max[:, None, None]), 0.0), axis=(1, 2)
    )
    stats = lax.all_gather(jnp.stack((local_max, local_sum)), "zz", axis=0)
    highest = jnp.max(stats[:, 0], axis=0)
    normalizer = jnp.sum(stats[:, 1] * jnp.exp(stats[:, 0] - highest[None, :]), axis=0)
    highest = jnp.where(g_alive, highest, 0.0)
    normalizer = jnp.where(g_alive, normalizer, 1.0)
    expo = jnp.where(mask[:, None, :], jnp.exp(score - highest[:, None, None]), 0.0)
    posterior = (expo / normalizer[:, None, None]).astype(jnp.bfloat16)
    posterior = jnp.where(g_alive[:, None, None], posterior, jnp.zeros_like(posterior))
    peak_all = jnp.where(g_alive, 1.0 / normalizer, 0.0)
    peak_weight = lax.dynamic_slice_in_dim(peak_all, zz * rows, rows, 0)

    flat_post = posterior.reshape(count, block)
    accum = lax.dot_general(
        flat_post, image_half, (((0,), (0,)), ((), ())), preferred_element_type=jnp.float32
    ).reshape(TRANS, chip_orients, PIX)
    a_real = accum[:, :, :COEF]
    a_imag = accum[:, :, COEF:]
    data_real = jnp.sum(c_t * a_real - s_t * a_imag, axis=0)
    data_imag = jnp.sum(s_t * a_real + c_t * a_imag, axis=0)
    data = jnp.concatenate((data_real, data_imag), axis=-1)

    per_orient = jnp.sum(posterior.astype(jnp.float32), axis=1)
    weight = lax.dot_general(
        per_orient, ctf_half.astype(jnp.float32), (((0,), (0,)), ((), ())), precision=HIGHEST
    )

    doms = lax.axis_size("dom")
    halves = lax.axis_size("cc")
    data_cols = PIX // doms
    weight_cols = COEF // doms
    data_b = data.reshape(halves, own_orients, doms, data_cols).transpose(0, 2, 1, 3)
    weight_b = weight.reshape(halves, own_orients, doms, weight_cols).transpose(0, 2, 1, 3)
    both = jnp.concatenate((data_b, weight_b), axis=-1).reshape(
        halves * doms * own_orients, data_cols + weight_cols
    )
    reduced = lax.psum_scatter(both, ("cc", "dom"), scatter_dimension=0, tiled=True)
    data_out = reduced[:, :data_cols]
    weight_out = reduced[:, data_cols:]
    return (peak_weight, data_out, weight_out)


def solution(mesh):
    doms = mesh.shape["dom"]
    slabs = mesh.shape["slab"]
    split = Mesh(mesh.devices.reshape(doms, slabs // 2, 2), ("dom", "zz", "cc"))
    rowwise = ("dom", "zz", "cc")
    placed = (
        P(rowwise, None),
        P(rowwise),
        P(),
        P(("zz", "cc"), None),
        P(rowwise, None),
        P(rowwise),
    )
    return jax.shard_map(
        shards,
        mesh=split,
        in_specs=placed,
        out_specs=(P(rowwise), P(("zz", "cc"), "dom"), P(("zz", "cc"), "dom")),
        check_vma=False,
    )
```

```python
import math

import numpy as np
import jax
import jax.numpy as jnp
from jax import lax
from jax.sharding import Mesh
from jax.sharding import PartitionSpec as P

SIDE = 64
COEF = 4096
PIX = 2 * COEF
TRANS = 25

SENTINEL = -1e30
HIGHEST = lax.Precision.HIGHEST


def _tables():
    position = np.arange(COEF)
    freq_x = (position // SIDE - SIDE // 2).astype(np.float64)
    freq_y = (position % SIDE - SIDE // 2).astype(np.float64)
    edge = math.isqrt(TRANS)
    half = edge // 2
    offsets = np.arange(TRANS)
    shift_x = (offsets // edge - half).astype(np.float64)
    shift_y = (offsets % edge - half).astype(np.float64)
    angle = 2.0 * np.pi * (shift_x[:, None] * freq_x[None, :] + shift_y[:, None] * freq_y[None, :]) / SIDE
    radius = (freq_x * freq_x + freq_y * freq_y) / (SIDE * SIDE)
    return (
        np.cos(angle).astype(np.float32),
        np.sin(angle).astype(np.float32),
        radius.astype(np.float32),
    )


COSINE, SINE, RADIUS = _tables()


def split3(values):
    first = values.astype(jnp.bfloat16)
    rest = values - first.astype(jnp.float32)
    second = rest.astype(jnp.bfloat16)
    third = (rest - second.astype(jnp.float32)).astype(jnp.bfloat16)
    return first, second, third


def ring_gather(values, axis, size):
    ahead = values
    behind = values
    later = []
    sooner = [values]
    for step in range(size // 2):
        ahead = lax.ppermute(ahead, axis, [(i, (i + 1) % size) for i in range(size)])
        later.append(ahead)
        if step < (size - 1) // 2:
            behind = lax.ppermute(behind, axis, [(i, (i - 1) % size) for i in range(size)])
            sooner.append(behind)
    return jnp.concatenate(sooner + later[::-1], axis=0)


def exchange(values, axis, size):
    spread = jnp.broadcast_to(values[None], (size,) + values.shape)
    return lax.all_to_all(spread, axis, 0, 0, tiled=True)


def shards(images, defocus, inv_noise, slices, lists, counts):
    rows = images.shape[0]
    own_orients = slices.shape[0]
    orient_total = own_orients * lax.axis_size("zz") * lax.axis_size("cc")
    pad = (-(orient_total + 2)) % 128
    zz = lax.axis_index("zz")
    cc = lax.axis_index("cc")

    orient_ids = jnp.arange(orient_total, dtype=jnp.int32)
    slot_live = jnp.arange(lists.shape[1], dtype=jnp.int32)[None, :] < counts[:, None]
    hits = (lists[:, :, None] == orient_ids[None, None, :]) & slot_live[:, :, None]
    mask_all = jnp.any(hits, axis=1)
    alive = counts > 0
    extra = jnp.concatenate(
        (
            mask_all.astype(jnp.bfloat16),
            alive.astype(jnp.bfloat16)[:, None],
            defocus[:, None],
            jnp.zeros((rows, pad), jnp.bfloat16),
        ),
        axis=1,
    )
    packed = jnp.concatenate((images, extra), axis=1)
    group = lax.axis_size("zz")
    gathered = ring_gather(packed, "zz", group)
    local_slices = lax.all_gather(slices, "cc", axis=0, tiled=True)
    count = gathered.shape[0]
    chip_orients = local_slices.shape[0]

    g_images = gathered[:, :PIX]
    g_mask_all = gathered[:, PIX : PIX + orient_total]
    g_alive = gathered[:, PIX + orient_total] > 0.5
    g_defocus = gathered[:, PIX + orient_total + 1].astype(jnp.float32)
    mask = lax.dynamic_slice_in_dim(g_mask_all, zz * chip_orients, chip_orients, 1) > 0.5

    cosine = jnp.asarray(COSINE)
    sine = jnp.asarray(SINE)
    radius = jnp.asarray(RADIUS)
    ctf = -jnp.sin(jnp.pi * g_defocus[:, None] * radius[None, :] + 0.1)
    real_part = g_images[:, :COEF].astype(jnp.float32)
    imag_part = g_images[:, COEF:].astype(jnp.float32)
    weighted = jnp.concatenate(
        (inv_noise * ctf * real_part, inv_noise * ctf * imag_part), axis=-1
    ).astype(jnp.bfloat16)
    image_half = jnp.concatenate((ctf * real_part, ctf * imag_part), axis=-1).astype(jnp.bfloat16)
    quad_half = (-0.5 * inv_noise * ctf * ctf).astype(jnp.bfloat16)
    ctf_half = (ctf * ctf).astype(jnp.bfloat16)
    weighted, image_half, quad_half, ctf_half = lax.optimization_barrier(
        (weighted, image_half, quad_half, ctf_half)
    )

    slices_wide = local_slices.astype(jnp.float32)
    squares = (slices_wide * slices_wide).astype(jnp.bfloat16)
    energy = lax.dot_general(
        quad_half, squares[:, :COEF], (((1,), (1,)), ((), ())), preferred_element_type=jnp.float32
    ) + lax.dot_general(
        quad_half, squares[:, COEF:], (((1,), (1,)), ((), ())), preferred_element_type=jnp.float32
    )

    s_real = slices_wide[None, :, :COEF]
    s_imag = slices_wide[None, :, COEF:]
    c_t = cosine[:, None, :]
    s_t = sine[:, None, :]
    turned = jnp.concatenate((c_t * s_real + s_t * s_imag, c_t * s_imag - s_t * s_real), axis=-1)
    turned = turned.reshape(TRANS * chip_orients, PIX)
    parts = jnp.concatenate(split3(turned), axis=0)
    linear3 = lax.dot_general(
        weighted, parts, (((1,), (1,)), ((), ())), preferred_element_type=jnp.float32
    )
    block = TRANS * chip_orients
    linear = linear3[:, :block] + linear3[:, block : 2 * block] + linear3[:, 2 * block :]
    linear = linear.reshape(count, TRANS, chip_orients)
    score = jnp.where(mask[:, None, :], linear + energy[:, None, :], SENTINEL)

    local_max = jnp.max(score, axis=(1, 2))
    local_sum = jnp.sum(
        jnp.where(mask[:, None, :], jnp.exp(score - local_max[:, None, None]), 0.0), axis=(1, 2)
    )
    shift = zz * rows
    stats = jnp.roll(jnp.stack((local_max, local_sum)), shift, axis=1)
    stats = exchange(stats, "zz", group)
    highest = jnp.roll(jnp.max(stats[:, 0], axis=0), -shift)
    normalizer = jnp.sum(stats[:, 1] * jnp.exp(stats[:, 0] - jnp.max(stats[:, 0], axis=0)[None, :]), axis=0)
    normalizer = jnp.roll(normalizer, -shift)
    highest = jnp.where(g_alive, highest, 0.0)
    normalizer = jnp.where(g_alive, normalizer, 1.0)
    expo = jnp.where(mask[:, None, :], jnp.exp(score - highest[:, None, None]), 0.0)
    posterior = (expo / normalizer[:, None, None]).astype(jnp.bfloat16)
    posterior = jnp.where(g_alive[:, None, None], posterior, jnp.zeros_like(posterior))
    peak_all = jnp.where(g_alive, 1.0 / normalizer, 0.0)
    peak_weight = peak_all[:rows]

    flat_post = posterior.reshape(count, block)
    accum = lax.dot_general(
        flat_post,
        jnp.concatenate((image_half, ctf_half), axis=1),
        (((0,), (0,)), ((), ())),
        preferred_element_type=jnp.float32,
    ).reshape(TRANS, chip_orients, PIX + COEF)
    weight = jnp.sum(accum[:, :, PIX:], axis=0)
    a_real = accum[:, :, :COEF]
    a_imag = accum[:, :, COEF:PIX]
    data_real = jnp.sum(c_t * a_real - s_t * a_imag, axis=0)
    data_imag = jnp.sum(s_t * a_real + c_t * a_imag, axis=0)
    data = jnp.concatenate((data_real, data_imag), axis=-1)


    doms = lax.axis_size("dom")
    halves = lax.axis_size("cc")
    data_cols = PIX // doms
    weight_cols = COEF // doms
    data_b = data.reshape(halves, own_orients, doms, data_cols).transpose(0, 2, 1, 3)
    weight_b = weight.reshape(halves, own_orients, doms, weight_cols).transpose(0, 2, 1, 3)
    both = jnp.concatenate((data_b, weight_b), axis=-1).reshape(
        halves * doms * own_orients, data_cols + weight_cols
    )
    pieces = halves * doms
    both = both.reshape(pieces, own_orients, data_cols + weight_cols)
    reduced = jnp.sum(lax.all_to_all(both, ("cc", "dom"), 0, 0, tiled=True), axis=0)
    data_out = reduced[:, :data_cols]
    weight_out = reduced[:, data_cols:]
    return (peak_weight, data_out, weight_out)


def solution(mesh):
    doms = mesh.shape["dom"]
    slabs = mesh.shape["slab"]
    split = Mesh(mesh.devices.reshape(doms, slabs // 2, 2), ("dom", "zz", "cc"))
    rowwise = ("dom", "zz", "cc")
    placed = (
        P(rowwise, None),
        P(rowwise),
        P(),
        P(("zz", "cc"), None),
        P(rowwise, None),
        P(rowwise),
    )
    return jax.shard_map(
        shards,
        mesh=split,
        in_specs=placed,
        out_specs=(P(rowwise), P(("zz", "cc"), "dom"), P(("zz", "cc"), "dom")),
        check_vma=False,
    )
```

```python
import math

import numpy as np
import jax
import jax.numpy as jnp
from jax import lax
from jax.sharding import Mesh
from jax.sharding import PartitionSpec as P

SIDE = 64
COEF = 4096
PIX = 2 * COEF
TRANS = 25

SENTINEL = -1e30
HIGHEST = lax.Precision.HIGHEST


def _tables():
    position = np.arange(COEF)
    freq_x = (position // SIDE - SIDE // 2).astype(np.float64)
    freq_y = (position % SIDE - SIDE // 2).astype(np.float64)
    edge = math.isqrt(TRANS)
    half = edge // 2
    offsets = np.arange(TRANS)
    shift_x = (offsets // edge - half).astype(np.float64)
    shift_y = (offsets % edge - half).astype(np.float64)
    angle = 2.0 * np.pi * (shift_x[:, None] * freq_x[None, :] + shift_y[:, None] * freq_y[None, :]) / SIDE
    radius = (freq_x * freq_x + freq_y * freq_y) / (SIDE * SIDE)
    return (
        np.cos(angle).astype(np.float32),
        np.sin(angle).astype(np.float32),
        radius.astype(np.float32),
    )


COSINE, SINE, RADIUS = _tables()


def split3(values):
    first = values.astype(jnp.bfloat16)
    rest = values - first.astype(jnp.float32)
    second = rest.astype(jnp.bfloat16)
    third = (rest - second.astype(jnp.float32)).astype(jnp.bfloat16)
    return first, second, third


def exchange(values, axis, size):
    spread = jnp.broadcast_to(values[None], (size,) + values.shape)
    return lax.all_to_all(spread, axis, 0, 0, tiled=True)


def shards(images, defocus, inv_noise, slices, lists, counts):
    rows = images.shape[0]
    own_orients = slices.shape[0]
    orient_total = own_orients * lax.axis_size("zz") * lax.axis_size("cc")
    pad = (-(orient_total + 2)) % 128
    zz = lax.axis_index("zz")
    cc = lax.axis_index("cc")

    orient_ids = jnp.arange(orient_total, dtype=jnp.int32)
    slot_live = jnp.arange(lists.shape[1], dtype=jnp.int32)[None, :] < counts[:, None]
    hits = (lists[:, :, None] == orient_ids[None, None, :]) & slot_live[:, :, None]
    mask_all = jnp.any(hits, axis=1)
    alive = counts > 0
    extra = jnp.concatenate(
        (
            mask_all.astype(jnp.bfloat16),
            alive.astype(jnp.bfloat16)[:, None],
            defocus[:, None],
            jnp.zeros((rows, pad), jnp.bfloat16),
        ),
        axis=1,
    )
    first = jnp.concatenate((images[:, :COEF], extra), axis=1)
    group = lax.axis_size("zz")
    gathered = lax.all_gather(first, "zz", axis=0, tiled=True)
    g_imag = lax.all_gather(images[:, COEF:], "zz", axis=0, tiled=True)
    local_slices = lax.all_gather(slices, "cc", axis=0, tiled=True)
    count = gathered.shape[0]
    chip_orients = local_slices.shape[0]

    g_mask_all = gathered[:, COEF : COEF + orient_total]
    g_alive = gathered[:, COEF + orient_total] > 0.5
    g_defocus = gathered[:, COEF + orient_total + 1].astype(jnp.float32)
    mask = lax.dynamic_slice_in_dim(g_mask_all, zz * chip_orients, chip_orients, 1) > 0.5

    cosine = jnp.asarray(COSINE)
    sine = jnp.asarray(SINE)
    radius = jnp.asarray(RADIUS)
    ctf = -jnp.sin(jnp.pi * g_defocus[:, None] * radius[None, :] + 0.1)
    quad_half = (-0.5 * inv_noise * ctf * ctf).astype(jnp.bfloat16)
    ctf_half = (ctf * ctf).astype(jnp.bfloat16)
    real_part = gathered[:, :COEF].astype(jnp.float32)
    weighted_r = (inv_noise * ctf * real_part).astype(jnp.bfloat16)
    image_r = (ctf * real_part).astype(jnp.bfloat16)
    ctf, weighted_r, image_r, quad_half, ctf_half = lax.optimization_barrier(
        (ctf, weighted_r, image_r, quad_half, ctf_half)
    )
    imag_part = g_imag.astype(jnp.float32)
    weighted_i = (inv_noise * ctf * imag_part).astype(jnp.bfloat16)
    image_i = (ctf * imag_part).astype(jnp.bfloat16)

    slices_wide = local_slices.astype(jnp.float32)
    squares = (slices_wide * slices_wide).astype(jnp.bfloat16)
    energy = lax.dot_general(
        quad_half, squares[:, :COEF], (((1,), (1,)), ((), ())), preferred_element_type=jnp.float32
    ) + lax.dot_general(
        quad_half, squares[:, COEF:], (((1,), (1,)), ((), ())), preferred_element_type=jnp.float32
    )

    s_real = slices_wide[None, :, :COEF]
    s_imag = slices_wide[None, :, COEF:]
    c_t = cosine[:, None, :]
    s_t = sine[:, None, :]
    block = TRANS * chip_orients
    turned_r = (c_t * s_real + s_t * s_imag).reshape(block, COEF)
    turned_i = (c_t * s_imag - s_t * s_real).reshape(block, COEF)
    parts_r = jnp.concatenate(split3(turned_r), axis=0)
    parts_i = jnp.concatenate(split3(turned_i), axis=0)
    linear3 = lax.dot_general(
        weighted_r, parts_r, (((1,), (1,)), ((), ())), preferred_element_type=jnp.float32
    ) + lax.dot_general(
        weighted_i, parts_i, (((1,), (1,)), ((), ())), preferred_element_type=jnp.float32
    )
    linear = linear3[:, :block] + linear3[:, block : 2 * block] + linear3[:, 2 * block :]
    linear = linear.reshape(count, TRANS, chip_orients)
    score = jnp.where(mask[:, None, :], linear + energy[:, None, :], SENTINEL)

    local_max = jnp.max(score, axis=(1, 2))
    local_sum = jnp.sum(
        jnp.where(mask[:, None, :], jnp.exp(score - local_max[:, None, None]), 0.0), axis=(1, 2)
    )
    stats = exchange(jnp.stack((local_max, local_sum)), "zz", group)
    highest = jnp.max(stats[:, 0], axis=0)
    normalizer = jnp.sum(stats[:, 1] * jnp.exp(stats[:, 0] - highest[None, :]), axis=0)
    highest = jnp.where(g_alive, highest, 0.0)
    normalizer = jnp.where(g_alive, normalizer, 1.0)
    expo = jnp.where(mask[:, None, :], jnp.exp(score - highest[:, None, None]), 0.0)
    posterior = (expo / normalizer[:, None, None]).astype(jnp.bfloat16)
    posterior = jnp.where(g_alive[:, None, None], posterior, jnp.zeros_like(posterior))
    peak_all = jnp.where(g_alive, 1.0 / normalizer, 0.0)
    peak_weight = lax.dynamic_slice_in_dim(peak_all, zz * rows, rows, 0)

    flat_post = posterior.reshape(count, block)
    accum = lax.dot_general(
        flat_post,
        jnp.concatenate((image_r, image_i, ctf_half), axis=1),
        (((0,), (0,)), ((), ())),
        preferred_element_type=jnp.float32,
    ).reshape(TRANS, chip_orients, PIX + COEF)
    weight = jnp.sum(accum[:, :, PIX:], axis=0)
    a_real = accum[:, :, :COEF]
    a_imag = accum[:, :, COEF:PIX]
    data_real = jnp.sum(c_t * a_real - s_t * a_imag, axis=0)
    data_imag = jnp.sum(s_t * a_real + c_t * a_imag, axis=0)
    data = jnp.concatenate((data_real, data_imag), axis=-1)


    doms = lax.axis_size("dom")
    halves = lax.axis_size("cc")
    data_cols = PIX // doms
    weight_cols = COEF // doms
    data_b = data.reshape(halves, own_orients, doms, data_cols).transpose(0, 2, 1, 3)
    weight_b = weight.reshape(halves, own_orients, doms, weight_cols).transpose(0, 2, 1, 3)
    both = jnp.concatenate((data_b, weight_b), axis=-1).reshape(
        halves * doms * own_orients, data_cols + weight_cols
    )
    pieces = halves * doms
    both = both.reshape(pieces, own_orients, data_cols + weight_cols)
    reduced = jnp.sum(lax.all_to_all(both, ("cc", "dom"), 0, 0, tiled=True), axis=0)
    data_out = reduced[:, :data_cols]
    weight_out = reduced[:, data_cols:]
    return (peak_weight, data_out, weight_out)


def solution(mesh):
    doms = mesh.shape["dom"]
    slabs = mesh.shape["slab"]
    split = Mesh(mesh.devices.reshape(doms, slabs // 2, 2), ("dom", "zz", "cc"))
    rowwise = ("dom", "zz", "cc")
    placed = (
        P(rowwise, None),
        P(rowwise),
        P(),
        P(("zz", "cc"), None),
        P(rowwise, None),
        P(rowwise),
    )
    return jax.shard_map(
        shards,
        mesh=split,
        in_specs=placed,
        out_specs=(P(rowwise), P(("zz", "cc"), "dom"), P(("zz", "cc"), "dom")),
        check_vma=False,
    )
```

```python
import math

import numpy as np
import jax
import jax.numpy as jnp
from jax import lax
from jax.sharding import Mesh
from jax.sharding import PartitionSpec as P

SIDE = 64
COEF = 4096
PIX = 2 * COEF
TRANS = 25

SENTINEL = -1e30
HIGHEST = lax.Precision.HIGHEST


def _tables():
    position = np.arange(COEF)
    freq_x = (position // SIDE - SIDE // 2).astype(np.float64)
    freq_y = (position % SIDE - SIDE // 2).astype(np.float64)
    edge = math.isqrt(TRANS)
    half = edge // 2
    offsets = np.arange(TRANS)
    shift_x = (offsets // edge - half).astype(np.float64)
    shift_y = (offsets % edge - half).astype(np.float64)
    angle = 2.0 * np.pi * (shift_x[:, None] * freq_x[None, :] + shift_y[:, None] * freq_y[None, :]) / SIDE
    radius = (freq_x * freq_x + freq_y * freq_y) / (SIDE * SIDE)
    return (
        np.cos(angle).astype(np.float32),
        np.sin(angle).astype(np.float32),
        radius.astype(np.float32),
    )


COSINE, SINE, RADIUS = _tables()


def split3(values):
    first = values.astype(jnp.bfloat16)
    rest = values - first.astype(jnp.float32)
    second = rest.astype(jnp.bfloat16)
    third = (rest - second.astype(jnp.float32)).astype(jnp.bfloat16)
    return first, second, third


def exchange(values, axis, size):
    spread = jnp.broadcast_to(values[None], (size,) + values.shape)
    return lax.all_to_all(spread, axis, 0, 0, tiled=True)


def shards(images, defocus, inv_noise, slices, lists, counts):
    rows = images.shape[0]
    own_orients = slices.shape[0]
    orient_total = own_orients * lax.axis_size("zz") * lax.axis_size("cc")
    pad = (-(orient_total + 2)) % 128
    zz = lax.axis_index("zz")
    cc = lax.axis_index("cc")

    orient_ids = jnp.arange(orient_total, dtype=jnp.int32)
    slot_live = jnp.arange(lists.shape[1], dtype=jnp.int32)[None, :] < counts[:, None]
    hits = (lists[:, :, None] == orient_ids[None, None, :]) & slot_live[:, :, None]
    mask_all = jnp.any(hits, axis=1)
    alive = counts > 0
    extra = jnp.concatenate(
        (
            mask_all.astype(jnp.bfloat16),
            alive.astype(jnp.bfloat16)[:, None],
            defocus[:, None],
            jnp.zeros((rows, pad), jnp.bfloat16),
        ),
        axis=1,
    )
    group = lax.axis_size("zz")
    meta = exchange(extra, "zz", group).reshape(group * rows, extra.shape[1])
    g_images = lax.all_gather(images, "zz", axis=0, tiled=True)
    local_slices = lax.all_gather(slices, "cc", axis=0, tiled=True)
    count = g_images.shape[0]
    chip_orients = local_slices.shape[0]

    g_mask_all = meta[:, :orient_total]
    g_alive = meta[:, orient_total] > 0.5
    g_defocus = meta[:, orient_total + 1].astype(jnp.float32)
    mask = lax.dynamic_slice_in_dim(g_mask_all, zz * chip_orients, chip_orients, 1) > 0.5

    cosine = jnp.asarray(COSINE)
    sine = jnp.asarray(SINE)
    radius = jnp.asarray(RADIUS)
    ctf = -jnp.sin(jnp.pi * g_defocus[:, None] * radius[None, :] + 0.1)
    quad_half = (-0.5 * inv_noise * ctf * ctf).astype(jnp.bfloat16)
    ctf_half = (ctf * ctf).astype(jnp.bfloat16)
    noise_ctf = inv_noise * ctf
    ctf, noise_ctf, quad_half, ctf_half = lax.optimization_barrier((ctf, noise_ctf, quad_half, ctf_half))
    real_part = g_images[:, :COEF].astype(jnp.float32)
    imag_part = g_images[:, COEF:].astype(jnp.float32)
    weighted_r = (noise_ctf * real_part).astype(jnp.bfloat16)
    weighted_i = (noise_ctf * imag_part).astype(jnp.bfloat16)
    image_r = (ctf * real_part).astype(jnp.bfloat16)
    image_i = (ctf * imag_part).astype(jnp.bfloat16)

    slices_wide = local_slices.astype(jnp.float32)
    squares = (slices_wide * slices_wide).astype(jnp.bfloat16)
    energy = lax.dot_general(
        quad_half, squares[:, :COEF], (((1,), (1,)), ((), ())), preferred_element_type=jnp.float32
    ) + lax.dot_general(
        quad_half, squares[:, COEF:], (((1,), (1,)), ((), ())), preferred_element_type=jnp.float32
    )

    s_real = slices_wide[None, :, :COEF]
    s_imag = slices_wide[None, :, COEF:]
    c_t = cosine[:, None, :]
    s_t = sine[:, None, :]
    block = TRANS * chip_orients
    turned_r = (c_t * s_real + s_t * s_imag).reshape(block, COEF)
    turned_i = (c_t * s_imag - s_t * s_real).reshape(block, COEF)
    parts_r = jnp.concatenate(split3(turned_r), axis=0)
    parts_i = jnp.concatenate(split3(turned_i), axis=0)
    linear3 = lax.dot_general(
        weighted_r, parts_r, (((1,), (1,)), ((), ())), preferred_element_type=jnp.float32
    ) + lax.dot_general(
        weighted_i, parts_i, (((1,), (1,)), ((), ())), preferred_element_type=jnp.float32
    )
    linear = linear3[:, :block] + linear3[:, block : 2 * block] + linear3[:, 2 * block :]
    linear = linear.reshape(count, TRANS, chip_orients)
    score = jnp.where(mask[:, None, :], linear + energy[:, None, :], SENTINEL)

    local_max = jnp.max(score, axis=(1, 2))
    local_sum = jnp.sum(
        jnp.where(mask[:, None, :], jnp.exp(score - local_max[:, None, None]), 0.0), axis=(1, 2)
    )
    stats = exchange(jnp.stack((local_max, local_sum)), "zz", group)
    highest = jnp.max(stats[:, 0], axis=0)
    normalizer = jnp.sum(stats[:, 1] * jnp.exp(stats[:, 0] - highest[None, :]), axis=0)
    highest = jnp.where(g_alive, highest, 0.0)
    normalizer = jnp.where(g_alive, normalizer, 1.0)
    expo = jnp.where(mask[:, None, :], jnp.exp(score - highest[:, None, None]), 0.0)
    posterior = (expo / normalizer[:, None, None]).astype(jnp.bfloat16)
    posterior = jnp.where(g_alive[:, None, None], posterior, jnp.zeros_like(posterior))
    peak_all = jnp.where(g_alive, 1.0 / normalizer, 0.0)
    peak_weight = lax.dynamic_slice_in_dim(peak_all, zz * rows, rows, 0)

    flat_post = posterior.reshape(count, block)
    accum = lax.dot_general(
        flat_post,
        jnp.concatenate((image_r, image_i, ctf_half), axis=1),
        (((0,), (0,)), ((), ())),
        preferred_element_type=jnp.float32,
    ).reshape(TRANS, chip_orients, PIX + COEF)
    weight = jnp.sum(accum[:, :, PIX:], axis=0)
    a_real = accum[:, :, :COEF]
    a_imag = accum[:, :, COEF:PIX]
    data_real = jnp.sum(c_t * a_real - s_t * a_imag, axis=0)
    data_imag = jnp.sum(s_t * a_real + c_t * a_imag, axis=0)
    data = jnp.concatenate((data_real, data_imag), axis=-1)


    doms = lax.axis_size("dom")
    halves = lax.axis_size("cc")
    data_cols = PIX // doms
    weight_cols = COEF // doms
    data_b = data.reshape(halves, own_orients, doms, data_cols).transpose(0, 2, 1, 3)
    weight_b = weight.reshape(halves, own_orients, doms, weight_cols).transpose(0, 2, 1, 3)
    both = jnp.concatenate((data_b, weight_b), axis=-1).reshape(
        halves * doms * own_orients, data_cols + weight_cols
    )
    pieces = halves * doms
    both = both.reshape(pieces, own_orients, data_cols + weight_cols)
    reduced = jnp.sum(lax.all_to_all(both, ("cc", "dom"), 0, 0, tiled=True), axis=0)
    data_out = reduced[:, :data_cols]
    weight_out = reduced[:, data_cols:]
    return (peak_weight, data_out, weight_out)


def solution(mesh):
    doms = mesh.shape["dom"]
    slabs = mesh.shape["slab"]
    split = Mesh(mesh.devices.reshape(doms, slabs // 2, 2), ("dom", "zz", "cc"))
    rowwise = ("dom", "zz", "cc")
    placed = (
        P(rowwise, None),
        P(rowwise),
        P(),
        P(("zz", "cc"), None),
        P(rowwise, None),
        P(rowwise),
    )
    return jax.shard_map(
        shards,
        mesh=split,
        in_specs=placed,
        out_specs=(P(rowwise), P(("zz", "cc"), "dom"), P(("zz", "cc"), "dom")),
        check_vma=False,
    )
```

```python
import math

import numpy as np
import jax
import jax.numpy as jnp
from jax import lax
from jax.sharding import Mesh
from jax.sharding import PartitionSpec as P

SIDE = 64
COEF = 4096
PIX = 2 * COEF
TRANS = 25

SENTINEL = -1e30
HIGHEST = lax.Precision.HIGHEST


def _tables():
    position = np.arange(COEF)
    freq_x = (position // SIDE - SIDE // 2).astype(np.float64)
    freq_y = (position % SIDE - SIDE // 2).astype(np.float64)
    edge = math.isqrt(TRANS)
    half = edge // 2
    offsets = np.arange(TRANS)
    shift_x = (offsets // edge - half).astype(np.float64)
    shift_y = (offsets % edge - half).astype(np.float64)
    angle = 2.0 * np.pi * (shift_x[:, None] * freq_x[None, :] + shift_y[:, None] * freq_y[None, :]) / SIDE
    radius = (freq_x * freq_x + freq_y * freq_y) / (SIDE * SIDE)
    return (
        np.cos(angle).astype(np.float32),
        np.sin(angle).astype(np.float32),
        radius.astype(np.float32),
    )


COSINE, SINE, RADIUS = _tables()


def split3(values):
    first = values.astype(jnp.bfloat16)
    rest = values - first.astype(jnp.float32)
    second = rest.astype(jnp.bfloat16)
    third = (rest - second.astype(jnp.float32)).astype(jnp.bfloat16)
    return first, second, third


def ring_blocks(values, axis, size):
    ahead = values
    behind = values
    later = []
    sooner = [values]
    for step in range(size // 2):
        ahead = lax.ppermute(ahead, axis, [(i, (i + 1) % size) for i in range(size)])
        later.append(ahead)
        if step < (size - 1) // 2:
            behind = lax.ppermute(behind, axis, [(i, (i - 1) % size) for i in range(size)])
            sooner.append(behind)
    return sooner + later[::-1]


def exchange(values, axis, size):
    spread = jnp.broadcast_to(values[None], (size,) + values.shape)
    return lax.all_to_all(spread, axis, 0, 0, tiled=True)


def shards(images, defocus, inv_noise, slices, lists, counts):
    rows = images.shape[0]
    own_orients = slices.shape[0]
    orient_total = own_orients * lax.axis_size("zz") * lax.axis_size("cc")
    pad = (-(orient_total + 2)) % 128
    zz = lax.axis_index("zz")
    cc = lax.axis_index("cc")

    orient_ids = jnp.arange(orient_total, dtype=jnp.int32)
    slot_live = jnp.arange(lists.shape[1], dtype=jnp.int32)[None, :] < counts[:, None]
    hits = (lists[:, :, None] == orient_ids[None, None, :]) & slot_live[:, :, None]
    mask_all = jnp.any(hits, axis=1)
    alive = counts > 0
    extra = jnp.concatenate(
        (
            mask_all.astype(jnp.bfloat16),
            alive.astype(jnp.bfloat16)[:, None],
            defocus[:, None],
            jnp.zeros((rows, pad), jnp.bfloat16),
        ),
        axis=1,
    )
    group = lax.axis_size("zz")
    shift = zz * rows
    meta = exchange(extra, "zz", group).reshape(group * rows, extra.shape[1])
    meta = jnp.roll(meta, -shift, axis=0)
    blocks = ring_blocks(images, "zz", group)
    local_slices = lax.all_gather(slices, "cc", axis=0, tiled=True)
    count = rows * group
    chip_orients = local_slices.shape[0]

    g_mask_all = meta[:, :orient_total]
    g_alive = meta[:, orient_total] > 0.5
    g_defocus = meta[:, orient_total + 1].astype(jnp.float32)
    mask = lax.dynamic_slice_in_dim(g_mask_all, zz * chip_orients, chip_orients, 1) > 0.5

    cosine = jnp.asarray(COSINE)
    sine = jnp.asarray(SINE)
    radius = jnp.asarray(RADIUS)
    ctf = -jnp.sin(jnp.pi * g_defocus[:, None] * radius[None, :] + 0.1)
    quad_half = (-0.5 * inv_noise * ctf * ctf).astype(jnp.bfloat16)
    ctf_half = (ctf * ctf).astype(jnp.bfloat16)
    noise_ctf = inv_noise * ctf
    ctf, noise_ctf, quad_half, ctf_half = lax.optimization_barrier((ctf, noise_ctf, quad_half, ctf_half))
    real_part = jnp.concatenate([b[:, :COEF] for b in blocks], axis=0).astype(jnp.float32)
    imag_part = jnp.concatenate([b[:, COEF:] for b in blocks], axis=0).astype(jnp.float32)
    weighted_r = (noise_ctf * real_part).astype(jnp.bfloat16)
    weighted_i = (noise_ctf * imag_part).astype(jnp.bfloat16)
    image_r = (ctf * real_part).astype(jnp.bfloat16)
    image_i = (ctf * imag_part).astype(jnp.bfloat16)

    slices_wide = local_slices.astype(jnp.float32)
    squares = (slices_wide * slices_wide).astype(jnp.bfloat16)
    energy = lax.dot_general(
        quad_half, squares[:, :COEF], (((1,), (1,)), ((), ())), preferred_element_type=jnp.float32
    ) + lax.dot_general(
        quad_half, squares[:, COEF:], (((1,), (1,)), ((), ())), preferred_element_type=jnp.float32
    )

    s_real = slices_wide[None, :, :COEF]
    s_imag = slices_wide[None, :, COEF:]
    c_t = cosine[:, None, :]
    s_t = sine[:, None, :]
    block = TRANS * chip_orients
    turned_r = (c_t * s_real + s_t * s_imag).reshape(block, COEF)
    turned_i = (c_t * s_imag - s_t * s_real).reshape(block, COEF)
    parts_r = jnp.concatenate(split3(turned_r), axis=0)
    parts_i = jnp.concatenate(split3(turned_i), axis=0)
    linear3 = lax.dot_general(
        weighted_r, parts_r, (((1,), (1,)), ((), ())), preferred_element_type=jnp.float32
    ) + lax.dot_general(
        weighted_i, parts_i, (((1,), (1,)), ((), ())), preferred_element_type=jnp.float32
    )
    linear = linear3[:, :block] + linear3[:, block : 2 * block] + linear3[:, 2 * block :]
    linear = linear.reshape(count, TRANS, chip_orients)
    score = jnp.where(mask[:, None, :], linear + energy[:, None, :], SENTINEL)

    local_max = jnp.max(score, axis=(1, 2))
    local_sum = jnp.sum(
        jnp.where(mask[:, None, :], jnp.exp(score - local_max[:, None, None]), 0.0), axis=(1, 2)
    )
    stats = exchange(jnp.roll(jnp.stack((local_max, local_sum)), shift, axis=1), "zz", group)
    top = jnp.max(stats[:, 0], axis=0)
    normalizer = jnp.roll(jnp.sum(stats[:, 1] * jnp.exp(stats[:, 0] - top[None, :]), axis=0), -shift)
    highest = jnp.roll(top, -shift)
    highest = jnp.where(g_alive, highest, 0.0)
    normalizer = jnp.where(g_alive, normalizer, 1.0)
    expo = jnp.where(mask[:, None, :], jnp.exp(score - highest[:, None, None]), 0.0)
    posterior = (expo / normalizer[:, None, None]).astype(jnp.bfloat16)
    posterior = jnp.where(g_alive[:, None, None], posterior, jnp.zeros_like(posterior))
    peak_all = jnp.where(g_alive, 1.0 / normalizer, 0.0)
    peak_weight = peak_all[:rows]

    flat_post = posterior.reshape(count, block)
    accum = lax.dot_general(
        flat_post,
        jnp.concatenate((image_r, image_i, ctf_half), axis=1),
        (((0,), (0,)), ((), ())),
        preferred_element_type=jnp.float32,
    ).reshape(TRANS, chip_orients, PIX + COEF)
    weight = jnp.sum(accum[:, :, PIX:], axis=0)
    a_real = accum[:, :, :COEF]
    a_imag = accum[:, :, COEF:PIX]
    data_real = jnp.sum(c_t * a_real - s_t * a_imag, axis=0)
    data_imag = jnp.sum(s_t * a_real + c_t * a_imag, axis=0)
    data = jnp.concatenate((data_real, data_imag), axis=-1)


    doms = lax.axis_size("dom")
    halves = lax.axis_size("cc")
    data_cols = PIX // doms
    weight_cols = COEF // doms
    data_b = data.reshape(halves, own_orients, doms, data_cols).transpose(0, 2, 1, 3)
    weight_b = weight.reshape(halves, own_orients, doms, weight_cols).transpose(0, 2, 1, 3)
    both = jnp.concatenate((data_b, weight_b), axis=-1).reshape(
        halves * doms * own_orients, data_cols + weight_cols
    )
    pieces = halves * doms
    both = both.reshape(pieces, own_orients, data_cols + weight_cols)
    moved = lax.all_to_all(both.astype(jnp.bfloat16), ("cc", "dom"), 0, 0, tiled=True)
    reduced = jnp.sum(moved.astype(jnp.float32), axis=0)
    data_out = reduced[:, :data_cols]
    weight_out = reduced[:, data_cols:]
    return (peak_weight, data_out, weight_out)


def solution(mesh):
    doms = mesh.shape["dom"]
    slabs = mesh.shape["slab"]
    split = Mesh(mesh.devices.reshape(doms, slabs // 2, 2), ("dom", "zz", "cc"))
    rowwise = ("dom", "zz", "cc")
    placed = (
        P(rowwise, None),
        P(rowwise),
        P(),
        P(("zz", "cc"), None),
        P(rowwise, None),
        P(rowwise),
    )
    return jax.shard_map(
        shards,
        mesh=split,
        in_specs=placed,
        out_specs=(P(rowwise), P(("zz", "cc"), "dom"), P(("zz", "cc"), "dom")),
        check_vma=False,
    )
```

```python
import math

import numpy as np
import jax
import jax.numpy as jnp
from jax import lax
from jax.sharding import Mesh
from jax.sharding import PartitionSpec as P

SIDE = 64
COEF = 4096
PIX = 2 * COEF
TRANS = 25

SENTINEL = -1e30
HIGHEST = lax.Precision.HIGHEST


def _tables():
    position = np.arange(COEF)
    freq_x = (position // SIDE - SIDE // 2).astype(np.float64)
    freq_y = (position % SIDE - SIDE // 2).astype(np.float64)
    edge = math.isqrt(TRANS)
    half = edge // 2
    offsets = np.arange(TRANS)
    shift_x = (offsets // edge - half).astype(np.float64)
    shift_y = (offsets % edge - half).astype(np.float64)
    angle = 2.0 * np.pi * (shift_x[:, None] * freq_x[None, :] + shift_y[:, None] * freq_y[None, :]) / SIDE
    radius = (freq_x * freq_x + freq_y * freq_y) / (SIDE * SIDE)
    return (
        np.cos(angle).astype(np.float32),
        np.sin(angle).astype(np.float32),
        radius.astype(np.float32),
    )


COSINE, SINE, RADIUS = _tables()


def split3(values):
    first = values.astype(jnp.bfloat16)
    rest = values - first.astype(jnp.float32)
    second = rest.astype(jnp.bfloat16)
    third = (rest - second.astype(jnp.float32)).astype(jnp.bfloat16)
    return first, second, third


def exchange(values, axis, size):
    spread = jnp.broadcast_to(values[None], (size,) + values.shape)
    return lax.all_to_all(spread, axis, 0, 0, tiled=True)


def shards(images, defocus, inv_noise, slices, lists, counts):
    rows = images.shape[0]
    own_orients = slices.shape[0]
    orient_total = own_orients * lax.axis_size("zz") * lax.axis_size("cc")
    pad = (-(orient_total + 2)) % 128
    zz = lax.axis_index("zz")
    cc = lax.axis_index("cc")

    orient_ids = jnp.arange(orient_total, dtype=jnp.int32)
    slot_live = jnp.arange(lists.shape[1], dtype=jnp.int32)[None, :] < counts[:, None]
    hits = (lists[:, :, None] == orient_ids[None, None, :]) & slot_live[:, :, None]
    mask_all = jnp.any(hits, axis=1)
    alive = counts > 0
    extra = jnp.concatenate(
        (
            mask_all.astype(jnp.bfloat16),
            alive.astype(jnp.bfloat16)[:, None],
            defocus[:, None],
            jnp.zeros((rows, pad), jnp.bfloat16),
        ),
        axis=1,
    )
    group = lax.axis_size("zz")
    shift = zz * rows
    meta = exchange(extra, "zz", group).reshape(group * rows, extra.shape[1])
    meta = jnp.roll(meta, -shift, axis=0)
    local_slices = lax.all_gather(slices, "cc", axis=0, tiled=True)
    up = [(i, (i + 1) % group) for i in range(group)]
    down = [(i, (i - 1) % group) for i in range(group)]
    ahead1 = lax.ppermute(images, "zz", up)
    behind1 = lax.ppermute(images, "zz", down)
    ahead1, behind1, local_slices = lax.optimization_barrier((ahead1, behind1, local_slices))
    ahead2 = lax.ppermute(ahead1, "zz", up)
    behind2 = lax.ppermute(behind1, "zz", down)
    ahead2, behind2, meta = lax.optimization_barrier((ahead2, behind2, meta))
    ahead3 = lax.ppermute(ahead2, "zz", up)
    behind3 = lax.ppermute(behind2, "zz", down)
    ahead4 = lax.ppermute(ahead3, "zz", up)
    blocks = [images, behind1, behind2, behind3, ahead4, ahead3, ahead2, ahead1]
    count = rows * group
    chip_orients = local_slices.shape[0]

    g_mask_all = meta[:, :orient_total]
    g_alive = meta[:, orient_total] > 0.5
    g_defocus = meta[:, orient_total + 1].astype(jnp.float32)
    mask = lax.dynamic_slice_in_dim(g_mask_all, zz * chip_orients, chip_orients, 1) > 0.5

    cosine = jnp.asarray(COSINE)
    sine = jnp.asarray(SINE)
    radius = jnp.asarray(RADIUS)
    ctf = -jnp.sin(jnp.pi * g_defocus[:, None] * radius[None, :] + 0.1)
    quad_half = (-0.5 * inv_noise * ctf * ctf).astype(jnp.bfloat16)
    ctf_half = (ctf * ctf).astype(jnp.bfloat16)
    noise_ctf = inv_noise * ctf
    ctf, noise_ctf, quad_half, ctf_half = lax.optimization_barrier((ctf, noise_ctf, quad_half, ctf_half))
    real_part = jnp.concatenate([b[:, :COEF] for b in blocks], axis=0).astype(jnp.float32)
    imag_part = jnp.concatenate([b[:, COEF:] for b in blocks], axis=0).astype(jnp.float32)
    weighted_r = (noise_ctf * real_part).astype(jnp.bfloat16)
    weighted_i = (noise_ctf * imag_part).astype(jnp.bfloat16)
    image_r = (ctf * real_part).astype(jnp.bfloat16)
    image_i = (ctf * imag_part).astype(jnp.bfloat16)

    slices_wide = local_slices.astype(jnp.float32)
    squares = (slices_wide * slices_wide).astype(jnp.bfloat16)
    energy = lax.dot_general(
        quad_half, squares[:, :COEF], (((1,), (1,)), ((), ())), preferred_element_type=jnp.float32
    ) + lax.dot_general(
        quad_half, squares[:, COEF:], (((1,), (1,)), ((), ())), preferred_element_type=jnp.float32
    )

    s_real = slices_wide[None, :, :COEF]
    s_imag = slices_wide[None, :, COEF:]
    c_t = cosine[:, None, :]
    s_t = sine[:, None, :]
    block = TRANS * chip_orients
    turned_r = (c_t * s_real + s_t * s_imag).reshape(block, COEF)
    turned_i = (c_t * s_imag - s_t * s_real).reshape(block, COEF)
    parts_r = jnp.concatenate(split3(turned_r), axis=0)
    parts_i = jnp.concatenate(split3(turned_i), axis=0)
    linear3 = lax.dot_general(
        weighted_r, parts_r, (((1,), (1,)), ((), ())), preferred_element_type=jnp.float32
    ) + lax.dot_general(
        weighted_i, parts_i, (((1,), (1,)), ((), ())), preferred_element_type=jnp.float32
    )
    linear = linear3[:, :block] + linear3[:, block : 2 * block] + linear3[:, 2 * block :]
    linear = linear.reshape(count, TRANS, chip_orients)
    score = jnp.where(mask[:, None, :], linear + energy[:, None, :], SENTINEL)

    local_max = jnp.max(score, axis=(1, 2))
    local_sum = jnp.sum(
        jnp.where(mask[:, None, :], jnp.exp(score - local_max[:, None, None]), 0.0), axis=(1, 2)
    )
    stats = exchange(jnp.roll(jnp.stack((local_max, local_sum)), shift, axis=1), "zz", group)
    top = jnp.max(stats[:, 0], axis=0)
    normalizer = jnp.roll(jnp.sum(stats[:, 1] * jnp.exp(stats[:, 0] - top[None, :]), axis=0), -shift)
    highest = jnp.roll(top, -shift)
    highest = jnp.where(g_alive, highest, 0.0)
    normalizer = jnp.where(g_alive, normalizer, 1.0)
    expo = jnp.where(mask[:, None, :], jnp.exp(score - highest[:, None, None]), 0.0)
    posterior = (expo / normalizer[:, None, None]).astype(jnp.bfloat16)
    posterior = jnp.where(g_alive[:, None, None], posterior, jnp.zeros_like(posterior))
    peak_all = jnp.where(g_alive, 1.0 / normalizer, 0.0)
    peak_weight = peak_all[:rows]

    flat_post = posterior.reshape(count, block)
    accum = lax.dot_general(
        flat_post,
        jnp.concatenate((image_r, image_i, ctf_half), axis=1),
        (((0,), (0,)), ((), ())),
        preferred_element_type=jnp.float32,
    ).reshape(TRANS, chip_orients, PIX + COEF)
    weight = jnp.sum(accum[:, :, PIX:], axis=0)
    a_real = accum[:, :, :COEF]
    a_imag = accum[:, :, COEF:PIX]
    data_real = jnp.sum(c_t * a_real - s_t * a_imag, axis=0)
    data_imag = jnp.sum(s_t * a_real + c_t * a_imag, axis=0)
    data = jnp.concatenate((data_real, data_imag), axis=-1)


    doms = lax.axis_size("dom")
    halves = lax.axis_size("cc")
    data_cols = PIX // doms
    weight_cols = COEF // doms
    data_b = data.reshape(halves, own_orients, doms, data_cols).transpose(0, 2, 1, 3)
    weight_b = weight.reshape(halves, own_orients, doms, weight_cols).transpose(0, 2, 1, 3)
    both = jnp.concatenate((data_b, weight_b), axis=-1).reshape(
        halves * doms * own_orients, data_cols + weight_cols
    )
    pieces = halves * doms
    both = both.reshape(pieces, own_orients, data_cols + weight_cols)
    moved = lax.all_to_all(both.astype(jnp.bfloat16), ("cc", "dom"), 0, 0, tiled=True)
    reduced = jnp.sum(moved.astype(jnp.float32), axis=0)
    data_out = reduced[:, :data_cols]
    weight_out = reduced[:, data_cols:]
    return (peak_weight, data_out, weight_out)


def solution(mesh):
    doms = mesh.shape["dom"]
    slabs = mesh.shape["slab"]
    split = Mesh(mesh.devices.reshape(doms, slabs // 2, 2), ("dom", "zz", "cc"))
    rowwise = ("dom", "zz", "cc")
    placed = (
        P(rowwise, None),
        P(rowwise),
        P(),
        P(("zz", "cc"), None),
        P(rowwise, None),
        P(rowwise),
    )
    return jax.shard_map(
        shards,
        mesh=split,
        in_specs=placed,
        out_specs=(P(rowwise), P(("zz", "cc"), "dom"), P(("zz", "cc"), "dom")),
        check_vma=False,
    )
```

```python
import math

import numpy as np
import jax
import jax.numpy as jnp
from jax import lax
from jax.sharding import Mesh
from jax.sharding import PartitionSpec as P

SIDE = 64
COEF = 4096
PIX = 2 * COEF
TRANS = 25

SENTINEL = -1e30
HIGHEST = lax.Precision.HIGHEST


def _tables():
    position = np.arange(COEF)
    freq_x = (position // SIDE - SIDE // 2).astype(np.float64)
    freq_y = (position % SIDE - SIDE // 2).astype(np.float64)
    edge = math.isqrt(TRANS)
    half = edge // 2
    offsets = np.arange(TRANS)
    shift_x = (offsets // edge - half).astype(np.float64)
    shift_y = (offsets % edge - half).astype(np.float64)
    angle = 2.0 * np.pi * (shift_x[:, None] * freq_x[None, :] + shift_y[:, None] * freq_y[None, :]) / SIDE
    radius = (freq_x * freq_x + freq_y * freq_y) / (SIDE * SIDE)
    return (
        np.cos(angle).astype(np.float32),
        np.sin(angle).astype(np.float32),
        radius.astype(np.float32),
    )


COSINE, SINE, RADIUS = _tables()


def split3(values):
    first = values.astype(jnp.bfloat16)
    rest = values - first.astype(jnp.float32)
    second = rest.astype(jnp.bfloat16)
    third = (rest - second.astype(jnp.float32)).astype(jnp.bfloat16)
    return first, second, third


def exchange(values, axis, size):
    spread = jnp.broadcast_to(values[None], (size,) + values.shape)
    return lax.all_to_all(spread, axis, 0, 0, tiled=True)


def shards(images, defocus, inv_noise, slices, lists, counts):
    rows = images.shape[0]
    own_orients = slices.shape[0]
    orient_total = own_orients * lax.axis_size("zz") * lax.axis_size("cc")
    pad = (-(orient_total + 2)) % 128
    zz = lax.axis_index("zz")
    cc = lax.axis_index("cc")

    orient_ids = jnp.arange(orient_total, dtype=jnp.int32)
    slot_live = jnp.arange(lists.shape[1], dtype=jnp.int32)[None, :] < counts[:, None]
    hits = (lists[:, :, None] == orient_ids[None, None, :]) & slot_live[:, :, None]
    mask_all = jnp.any(hits, axis=1)
    alive = counts > 0
    extra = jnp.concatenate(
        (
            mask_all.astype(jnp.bfloat16),
            alive.astype(jnp.bfloat16)[:, None],
            defocus[:, None],
            jnp.zeros((rows, pad), jnp.bfloat16),
        ),
        axis=1,
    )
    group = lax.axis_size("zz")
    meta = exchange(extra, "zz", group).reshape(group * rows, extra.shape[1])
    g_images = lax.all_gather(images, "zz", axis=0, tiled=True)
    local_slices = lax.all_gather(slices, "cc", axis=0, tiled=True)
    count = g_images.shape[0]
    chip_orients = local_slices.shape[0]

    g_mask_all = meta[:, :orient_total]
    g_alive = meta[:, orient_total] > 0.5
    g_defocus = meta[:, orient_total + 1].astype(jnp.float32)
    mask = lax.dynamic_slice_in_dim(g_mask_all, zz * chip_orients, chip_orients, 1) > 0.5

    cosine = jnp.asarray(COSINE)
    sine = jnp.asarray(SINE)
    radius = jnp.asarray(RADIUS)
    ctf = -jnp.sin(jnp.pi * g_defocus[:, None] * radius[None, :] + 0.1)
    quad_half = (-0.5 * inv_noise * ctf * ctf).astype(jnp.bfloat16)
    ctf_half = (ctf * ctf).astype(jnp.bfloat16)
    noise_ctf = inv_noise * ctf
    ctf, noise_ctf, quad_half, ctf_half = lax.optimization_barrier((ctf, noise_ctf, quad_half, ctf_half))
    real_part = g_images[:, :COEF].astype(jnp.float32)
    imag_part = g_images[:, COEF:].astype(jnp.float32)
    weighted_r = (noise_ctf * real_part).astype(jnp.bfloat16)
    weighted_i = (noise_ctf * imag_part).astype(jnp.bfloat16)
    image_r = (ctf * real_part).astype(jnp.bfloat16)
    image_i = (ctf * imag_part).astype(jnp.bfloat16)

    slices_wide = local_slices.astype(jnp.float32)
    squares = (slices_wide * slices_wide).astype(jnp.bfloat16)
    energy = lax.dot_general(
        quad_half, squares[:, :COEF], (((1,), (1,)), ((), ())), preferred_element_type=jnp.float32
    ) + lax.dot_general(
        quad_half, squares[:, COEF:], (((1,), (1,)), ((), ())), preferred_element_type=jnp.float32
    )

    s_real = slices_wide[None, :, :COEF]
    s_imag = slices_wide[None, :, COEF:]
    c_t = cosine[:, None, :]
    s_t = sine[:, None, :]
    block = TRANS * chip_orients
    turned_r = (c_t * s_real + s_t * s_imag).reshape(block, COEF)
    turned_i = (c_t * s_imag - s_t * s_real).reshape(block, COEF)
    parts_r = jnp.concatenate(split3(turned_r), axis=0)
    parts_i = jnp.concatenate(split3(turned_i), axis=0)
    linear3 = lax.dot_general(
        weighted_r, parts_r, (((1,), (1,)), ((), ())), preferred_element_type=jnp.float32
    ) + lax.dot_general(
        weighted_i, parts_i, (((1,), (1,)), ((), ())), preferred_element_type=jnp.float32
    )
    linear = linear3[:, :block] + linear3[:, block : 2 * block] + linear3[:, 2 * block :]
    linear = linear.reshape(count, TRANS, chip_orients)
    score = jnp.where(mask[:, None, :], linear + energy[:, None, :], SENTINEL)

    local_max = jnp.max(score, axis=(1, 2))
    local_sum = jnp.sum(
        jnp.where(mask[:, None, :], jnp.exp(score - local_max[:, None, None]), 0.0), axis=(1, 2)
    )
    stats = exchange(jnp.stack((local_max, local_sum)), "zz", group)
    highest = jnp.max(stats[:, 0], axis=0)
    normalizer = jnp.sum(stats[:, 1] * jnp.exp(stats[:, 0] - highest[None, :]), axis=0)
    highest = jnp.where(g_alive, highest, 0.0)
    normalizer = jnp.where(g_alive, normalizer, 1.0)
    expo = jnp.where(mask[:, None, :], jnp.exp(score - highest[:, None, None]), 0.0)
    posterior = (expo / normalizer[:, None, None]).astype(jnp.bfloat16)
    posterior = jnp.where(g_alive[:, None, None], posterior, jnp.zeros_like(posterior))
    peak_all = jnp.where(g_alive, 1.0 / normalizer, 0.0)
    peak_weight = lax.dynamic_slice_in_dim(peak_all, zz * rows, rows, 0)

    flat_post = posterior.reshape(count, block)
    accum = lax.dot_general(
        flat_post,
        jnp.concatenate((image_r, image_i, ctf_half), axis=1),
        (((0,), (0,)), ((), ())),
        preferred_element_type=jnp.float32,
    ).reshape(TRANS, chip_orients, PIX + COEF)
    weight = jnp.sum(accum[:, :, PIX:], axis=0)
    a_real = accum[:, :, :COEF]
    a_imag = accum[:, :, COEF:PIX]
    data_real = jnp.sum(c_t * a_real - s_t * a_imag, axis=0)
    data_imag = jnp.sum(s_t * a_real + c_t * a_imag, axis=0)
    data = jnp.concatenate((data_real, data_imag), axis=-1)


    doms = lax.axis_size("dom")
    halves = lax.axis_size("cc")
    data_cols = PIX // doms
    weight_cols = COEF // doms
    data_b = data.reshape(halves, own_orients, doms, data_cols).transpose(0, 2, 1, 3)
    weight_b = weight.reshape(halves, own_orients, doms, weight_cols).transpose(0, 2, 1, 3)
    both = jnp.concatenate((data_b, weight_b), axis=-1).reshape(
        halves * doms * own_orients, data_cols + weight_cols
    )
    pieces = halves * doms
    both = both.reshape(pieces, own_orients, data_cols + weight_cols)
    moved = lax.all_to_all(both.astype(jnp.bfloat16), ("cc", "dom"), 0, 0, tiled=True)
    reduced = jnp.sum(moved.astype(jnp.float32), axis=0)
    data_out = reduced[:, :data_cols]
    weight_out = reduced[:, data_cols:]
    return (peak_weight, data_out, weight_out)


def solution(mesh):
    doms = mesh.shape["dom"]
    slabs = mesh.shape["slab"]
    split = Mesh(mesh.devices.reshape(doms, slabs // 2, 2), ("dom", "zz", "cc"))
    rowwise = ("dom", "zz", "cc")
    placed = (
        P(rowwise, None),
        P(rowwise),
        P(),
        P(("zz", "cc"), None),
        P(rowwise, None),
        P(rowwise),
    )
    return jax.shard_map(
        shards,
        mesh=split,
        in_specs=placed,
        out_specs=(P(rowwise), P(("zz", "cc"), "dom"), P(("zz", "cc"), "dom")),
        check_vma=False,
    )
```

```python
import math

import numpy as np
import jax
import jax.numpy as jnp
from jax import lax
from jax.sharding import Mesh
from jax.sharding import PartitionSpec as P

SIDE = 64
COEF = 4096
PIX = 2 * COEF
TRANS = 25

SENTINEL = -1e30
HIGHEST = lax.Precision.HIGHEST


def _tables():
    position = np.arange(COEF)
    freq_x = (position // SIDE - SIDE // 2).astype(np.float64)
    freq_y = (position % SIDE - SIDE // 2).astype(np.float64)
    edge = math.isqrt(TRANS)
    half = edge // 2
    offsets = np.arange(TRANS)
    shift_x = (offsets // edge - half).astype(np.float64)
    shift_y = (offsets % edge - half).astype(np.float64)
    angle = 2.0 * np.pi * (shift_x[:, None] * freq_x[None, :] + shift_y[:, None] * freq_y[None, :]) / SIDE
    radius = (freq_x * freq_x + freq_y * freq_y) / (SIDE * SIDE)
    return (
        np.cos(angle).astype(np.float32),
        np.sin(angle).astype(np.float32),
        radius.astype(np.float32),
    )


COSINE, SINE, RADIUS = _tables()


def split3(values):
    first = values.astype(jnp.bfloat16)
    rest = values - first.astype(jnp.float32)
    second = rest.astype(jnp.bfloat16)
    third = (rest - second.astype(jnp.float32)).astype(jnp.bfloat16)
    return first, second, third


def exchange(values, axis, size):
    spread = jnp.broadcast_to(values[None], (size,) + values.shape)
    return lax.all_to_all(spread, axis, 0, 0, tiled=True)


def shards(images, defocus, inv_noise, slices, lists, counts):
    rows = images.shape[0]
    own_orients = slices.shape[0]
    orient_total = own_orients * lax.axis_size("zz") * lax.axis_size("cc")
    pad = (-(orient_total + 2)) % 128
    zz = lax.axis_index("zz")
    cc = lax.axis_index("cc")

    orient_ids = jnp.arange(orient_total, dtype=jnp.int32)
    slot_live = jnp.arange(lists.shape[1], dtype=jnp.int32)[None, :] < counts[:, None]
    hits = (lists[:, :, None] == orient_ids[None, None, :]) & slot_live[:, :, None]
    mask_all = jnp.any(hits, axis=1)
    alive = counts > 0
    extra = jnp.concatenate(
        (
            mask_all.astype(jnp.bfloat16),
            alive.astype(jnp.bfloat16)[:, None],
            defocus[:, None],
            jnp.zeros((rows, pad), jnp.bfloat16),
        ),
        axis=1,
    )
    group = lax.axis_size("zz")
    meta = exchange(extra, "zz", group).reshape(group * rows, extra.shape[1])
    g_images = lax.all_gather(images, "zz", axis=0, tiled=True)
    local_slices = lax.all_gather(slices, "cc", axis=0, tiled=True)
    count = g_images.shape[0]
    chip_orients = local_slices.shape[0]

    g_mask_all = meta[:, :orient_total]
    g_alive = meta[:, orient_total] > 0.5
    g_defocus = meta[:, orient_total + 1].astype(jnp.float32)
    mask = lax.dynamic_slice_in_dim(g_mask_all, zz * chip_orients, chip_orients, 1) > 0.5

    cosine = jnp.asarray(COSINE)
    sine = jnp.asarray(SINE)
    radius = jnp.asarray(RADIUS)
    ctf = -jnp.sin(jnp.pi * g_defocus[:, None] * radius[None, :] + 0.1)
    quad_half = (-0.5 * inv_noise * ctf * ctf).astype(jnp.bfloat16)
    ctf_half = (ctf * ctf).astype(jnp.bfloat16)
    noise_ctf = inv_noise * ctf
    ctf, noise_ctf, quad_half, ctf_half = lax.optimization_barrier((ctf, noise_ctf, quad_half, ctf_half))
    real_part = g_images[:, :COEF].astype(jnp.float32)
    imag_part = g_images[:, COEF:].astype(jnp.float32)
    weighted_r = (noise_ctf * real_part).astype(jnp.bfloat16)
    weighted_i = (noise_ctf * imag_part).astype(jnp.bfloat16)
    image_r = (ctf * real_part).astype(jnp.bfloat16)
    image_i = (ctf * imag_part).astype(jnp.bfloat16)

    slices_wide = local_slices.astype(jnp.float32)
    squares = (slices_wide * slices_wide).astype(jnp.bfloat16)
    energy = lax.dot_general(
        quad_half, squares[:, :COEF], (((1,), (1,)), ((), ())), preferred_element_type=jnp.float32
    ) + lax.dot_general(
        quad_half, squares[:, COEF:], (((1,), (1,)), ((), ())), preferred_element_type=jnp.float32
    )

    s_real = slices_wide[None, :, :COEF]
    s_imag = slices_wide[None, :, COEF:]
    c_t = cosine[:, None, :]
    s_t = sine[:, None, :]
    block = TRANS * chip_orients
    turned_r = (c_t * s_real + s_t * s_imag).reshape(block, COEF)
    turned_i = (c_t * s_imag - s_t * s_real).reshape(block, COEF)
    parts_r = jnp.concatenate(split3(turned_r), axis=0)
    parts_i = jnp.concatenate(split3(turned_i), axis=0)
    linear3 = lax.dot_general(
        weighted_r, parts_r, (((1,), (1,)), ((), ())), preferred_element_type=jnp.float32
    ) + lax.dot_general(
        weighted_i, parts_i, (((1,), (1,)), ((), ())), preferred_element_type=jnp.float32
    )
    linear = linear3[:, :block] + linear3[:, block : 2 * block] + linear3[:, 2 * block :]
    linear = linear.reshape(count, TRANS, chip_orients)
    score = jnp.where(mask[:, None, :], linear + energy[:, None, :], SENTINEL)

    local_max = jnp.max(score, axis=(1, 2))
    local_sum = jnp.sum(
        jnp.where(mask[:, None, :], jnp.exp(score - local_max[:, None, None]), 0.0), axis=(1, 2)
    )
    stats = exchange(jnp.stack((local_max, local_sum)), "zz", group)
    highest = jnp.max(stats[:, 0], axis=0)
    normalizer = jnp.sum(stats[:, 1] * jnp.exp(stats[:, 0] - highest[None, :]), axis=0)
    highest = jnp.where(g_alive, highest, 0.0)
    normalizer = jnp.where(g_alive, normalizer, 1.0)
    expo = jnp.where(mask[:, None, :], jnp.exp(score - highest[:, None, None]), 0.0)
    posterior = (expo / normalizer[:, None, None]).astype(jnp.bfloat16)
    posterior = jnp.where(g_alive[:, None, None], posterior, jnp.zeros_like(posterior))
    peak_all = jnp.where(g_alive, 1.0 / normalizer, 0.0)
    peak_weight = lax.dynamic_slice_in_dim(peak_all, zz * rows, rows, 0)

    flat_post = posterior.reshape(count, block)
    accum = lax.dot_general(
        flat_post,
        jnp.concatenate((image_r, image_i, ctf_half), axis=1),
        (((0,), (0,)), ((), ())),
        preferred_element_type=jnp.float32,
    ).reshape(TRANS, chip_orients, PIX + COEF)
    weight = jnp.sum(accum[:, :, PIX:], axis=0)
    a_real = accum[:, :, :COEF]
    a_imag = accum[:, :, COEF:PIX]
    data_real = jnp.sum(c_t * a_real - s_t * a_imag, axis=0)
    data_imag = jnp.sum(s_t * a_real + c_t * a_imag, axis=0)
    data = jnp.concatenate((data_real, data_imag), axis=-1)


    doms = lax.axis_size("dom")
    halves = lax.axis_size("cc")
    data_cols = PIX // doms
    weight_cols = COEF // doms
    data_b = data.reshape(halves, own_orients, doms, data_cols).transpose(0, 2, 1, 3)
    weight_b = weight.reshape(halves, own_orients, doms, weight_cols).transpose(0, 2, 1, 3)
    both = jnp.concatenate((data_b, weight_b), axis=-1).reshape(
        halves * doms * own_orients, data_cols + weight_cols
    )
    both = both.reshape(halves, doms, own_orients, data_cols + weight_cols)
    mine = lax.dynamic_index_in_dim(both, cc, 0, keepdims=False)
    other = lax.dynamic_index_in_dim(both, 1 - cc, 0, keepdims=False)
    paired = mine + lax.ppermute(other, "cc", [(0, 1), (1, 0)])
    reduced = jnp.sum(lax.all_to_all(paired, "dom", 0, 0, tiled=True), axis=0)
    data_out = reduced[:, :data_cols]
    weight_out = reduced[:, data_cols:]
    return (peak_weight, data_out, weight_out)


def solution(mesh):
    doms = mesh.shape["dom"]
    slabs = mesh.shape["slab"]
    split = Mesh(mesh.devices.reshape(doms, slabs // 2, 2), ("dom", "zz", "cc"))
    rowwise = ("dom", "zz", "cc")
    placed = (
        P(rowwise, None),
        P(rowwise),
        P(),
        P(("zz", "cc"), None),
        P(rowwise, None),
        P(rowwise),
    )
    return jax.shard_map(
        shards,
        mesh=split,
        in_specs=placed,
        out_specs=(P(rowwise), P(("zz", "cc"), "dom"), P(("zz", "cc"), "dom")),
        check_vma=False,
    )
```

```python
import math

import numpy as np
import jax
import jax.numpy as jnp
from jax import lax
from jax.sharding import Mesh
from jax.sharding import PartitionSpec as P

SIDE = 64
COEF = 4096
PIX = 2 * COEF
TRANS = 25

SENTINEL = -1e30
HIGHEST = lax.Precision.HIGHEST


def _tables():
    position = np.arange(COEF)
    freq_x = (position // SIDE - SIDE // 2).astype(np.float64)
    freq_y = (position % SIDE - SIDE // 2).astype(np.float64)
    edge = math.isqrt(TRANS)
    half = edge // 2
    offsets = np.arange(TRANS)
    shift_x = (offsets // edge - half).astype(np.float64)
    shift_y = (offsets % edge - half).astype(np.float64)
    angle = 2.0 * np.pi * (shift_x[:, None] * freq_x[None, :] + shift_y[:, None] * freq_y[None, :]) / SIDE
    radius = (freq_x * freq_x + freq_y * freq_y) / (SIDE * SIDE)
    return (
        np.cos(angle).astype(np.float32),
        np.sin(angle).astype(np.float32),
        radius.astype(np.float32),
    )


COSINE, SINE, RADIUS = _tables()


def split3(values):
    first = values.astype(jnp.bfloat16)
    rest = values - first.astype(jnp.float32)
    second = rest.astype(jnp.bfloat16)
    third = (rest - second.astype(jnp.float32)).astype(jnp.bfloat16)
    return first, second, third


def exchange(values, axis, size):
    spread = jnp.broadcast_to(values[None], (size,) + values.shape)
    return lax.all_to_all(spread, axis, 0, 0, tiled=True)


def shards(images, defocus, inv_noise, slices, lists, counts):
    rows = images.shape[0]
    own_orients = slices.shape[0]
    orient_total = own_orients * lax.axis_size("zz") * lax.axis_size("cc")
    pad = (-(orient_total + 2)) % 128
    zz = lax.axis_index("zz")
    cc = lax.axis_index("cc")

    orient_ids = jnp.arange(orient_total, dtype=jnp.int32)
    slot_live = jnp.arange(lists.shape[1], dtype=jnp.int32)[None, :] < counts[:, None]
    hits = (lists[:, :, None] == orient_ids[None, None, :]) & slot_live[:, :, None]
    mask_all = jnp.any(hits, axis=1)
    alive = counts > 0
    extra = jnp.concatenate(
        (
            mask_all.astype(jnp.bfloat16),
            alive.astype(jnp.bfloat16)[:, None],
            defocus[:, None],
            jnp.zeros((rows, pad), jnp.bfloat16),
        ),
        axis=1,
    )
    group = lax.axis_size("zz")
    meta = exchange(extra, "zz", group).reshape(group * rows, extra.shape[1])
    g_images = lax.all_gather(images, "zz", axis=0, tiled=True)
    local_slices = lax.all_gather(slices, "cc", axis=0, tiled=True)
    count = g_images.shape[0]
    chip_orients = local_slices.shape[0]

    g_mask_all = meta[:, :orient_total]
    g_alive = meta[:, orient_total] > 0.5
    g_defocus = meta[:, orient_total + 1].astype(jnp.float32)
    mask = lax.dynamic_slice_in_dim(g_mask_all, zz * chip_orients, chip_orients, 1) > 0.5

    cosine = jnp.asarray(COSINE)
    sine = jnp.asarray(SINE)
    radius = jnp.asarray(RADIUS)
    ctf = -jnp.sin(jnp.pi * g_defocus[:, None] * radius[None, :] + 0.1)
    quad_half = (-0.5 * inv_noise * ctf * ctf).astype(jnp.bfloat16)
    ctf_half = (ctf * ctf).astype(jnp.bfloat16)
    noise_ctf = inv_noise * ctf
    ctf, noise_ctf, quad_half, ctf_half = lax.optimization_barrier((ctf, noise_ctf, quad_half, ctf_half))
    real_part = g_images[:, :COEF].astype(jnp.float32)
    imag_part = g_images[:, COEF:].astype(jnp.float32)
    weighted_r = (noise_ctf * real_part).astype(jnp.bfloat16)
    weighted_i = (noise_ctf * imag_part).astype(jnp.bfloat16)
    image_r = (ctf * real_part).astype(jnp.bfloat16)
    image_i = (ctf * imag_part).astype(jnp.bfloat16)

    slices_wide = local_slices.astype(jnp.float32)
    squares = (slices_wide * slices_wide).astype(jnp.bfloat16)
    energy = lax.dot_general(
        quad_half, squares[:, :COEF], (((1,), (1,)), ((), ())), preferred_element_type=jnp.float32
    ) + lax.dot_general(
        quad_half, squares[:, COEF:], (((1,), (1,)), ((), ())), preferred_element_type=jnp.float32
    )

    s_real = slices_wide[None, :, :COEF]
    s_imag = slices_wide[None, :, COEF:]
    c_t = cosine[:, None, :]
    s_t = sine[:, None, :]
    block = TRANS * chip_orients
    turned_r = (c_t * s_real + s_t * s_imag).reshape(block, COEF)
    turned_i = (c_t * s_imag - s_t * s_real).reshape(block, COEF)
    parts_r = jnp.concatenate(split3(turned_r), axis=0)
    parts_i = jnp.concatenate(split3(turned_i), axis=0)
    linear3 = lax.dot_general(
        jnp.concatenate((weighted_r, weighted_i), axis=1),
        jnp.concatenate((parts_r, parts_i), axis=1),
        (((1,), (1,)), ((), ())),
        preferred_element_type=jnp.float32,
    )
    linear = linear3[:, :block] + linear3[:, block : 2 * block] + linear3[:, 2 * block :]
    linear = linear.reshape(count, TRANS, chip_orients)
    score = jnp.where(mask[:, None, :], linear + energy[:, None, :], SENTINEL)

    local_max = jnp.max(score, axis=(1, 2))
    local_sum = jnp.sum(
        jnp.where(mask[:, None, :], jnp.exp(score - local_max[:, None, None]), 0.0), axis=(1, 2)
    )
    stats = exchange(jnp.stack((local_max, local_sum)), "zz", group)
    highest = jnp.max(stats[:, 0], axis=0)
    normalizer = jnp.sum(stats[:, 1] * jnp.exp(stats[:, 0] - highest[None, :]), axis=0)
    highest = jnp.where(g_alive, highest, 0.0)
    normalizer = jnp.where(g_alive, normalizer, 1.0)
    expo = jnp.where(mask[:, None, :], jnp.exp(score - highest[:, None, None]), 0.0)
    posterior = (expo / normalizer[:, None, None]).astype(jnp.bfloat16)
    posterior = jnp.where(g_alive[:, None, None], posterior, jnp.zeros_like(posterior))
    peak_all = jnp.where(g_alive, 1.0 / normalizer, 0.0)
    peak_weight = lax.dynamic_slice_in_dim(peak_all, zz * rows, rows, 0)

    flat_post = posterior.reshape(count, block)
    accum = lax.dot_general(
        flat_post,
        jnp.concatenate((image_r, image_i, ctf_half), axis=1),
        (((0,), (0,)), ((), ())),
        preferred_element_type=jnp.float32,
    ).reshape(TRANS, chip_orients, PIX + COEF)
    weight = jnp.sum(accum[:, :, PIX:], axis=0)
    a_real = accum[:, :, :COEF]
    a_imag = accum[:, :, COEF:PIX]
    data_real = jnp.sum(c_t * a_real - s_t * a_imag, axis=0)
    data_imag = jnp.sum(s_t * a_real + c_t * a_imag, axis=0)
    data = jnp.concatenate((data_real, data_imag), axis=-1)


    doms = lax.axis_size("dom")
    halves = lax.axis_size("cc")
    data_cols = PIX // doms
    weight_cols = COEF // doms
    data_b = data.reshape(halves, own_orients, doms, data_cols).transpose(0, 2, 1, 3)
    weight_b = weight.reshape(halves, own_orients, doms, weight_cols).transpose(0, 2, 1, 3)
    both = jnp.concatenate((data_b, weight_b), axis=-1).reshape(
        halves * doms * own_orients, data_cols + weight_cols
    )
    both = both.reshape(halves, doms, own_orients, data_cols + weight_cols)
    mine = lax.dynamic_index_in_dim(both, cc, 0, keepdims=False)
    other = lax.dynamic_index_in_dim(both, 1 - cc, 0, keepdims=False)
    paired = mine + lax.ppermute(other, "cc", [(0, 1), (1, 0)])
    reduced = jnp.sum(lax.all_to_all(paired, "dom", 0, 0, tiled=True), axis=0)
    data_out = reduced[:, :data_cols]
    weight_out = reduced[:, data_cols:]
    return (peak_weight, data_out, weight_out)


def solution(mesh):
    doms = mesh.shape["dom"]
    slabs = mesh.shape["slab"]
    split = Mesh(mesh.devices.reshape(doms, slabs // 2, 2), ("dom", "zz", "cc"))
    rowwise = ("dom", "zz", "cc")
    placed = (
        P(rowwise, None),
        P(rowwise),
        P(),
        P(("zz", "cc"), None),
        P(rowwise, None),
        P(rowwise),
    )
    return jax.shard_map(
        shards,
        mesh=split,
        in_specs=placed,
        out_specs=(P(rowwise), P(("zz", "cc"), "dom"), P(("zz", "cc"), "dom")),
        check_vma=False,
    )
```

```python
import math

import numpy as np
import jax
import jax.numpy as jnp
from jax import lax
from jax.sharding import Mesh
from jax.sharding import PartitionSpec as P

SIDE = 64
COEF = 4096
PIX = 2 * COEF
TRANS = 25

SENTINEL = -1e30
HIGHEST = lax.Precision.HIGHEST


def _tables():
    position = np.arange(COEF)
    freq_x = (position // SIDE - SIDE // 2).astype(np.float64)
    freq_y = (position % SIDE - SIDE // 2).astype(np.float64)
    edge = math.isqrt(TRANS)
    half = edge // 2
    offsets = np.arange(TRANS)
    shift_x = (offsets // edge - half).astype(np.float64)
    shift_y = (offsets % edge - half).astype(np.float64)
    angle = 2.0 * np.pi * (shift_x[:, None] * freq_x[None, :] + shift_y[:, None] * freq_y[None, :]) / SIDE
    radius = (freq_x * freq_x + freq_y * freq_y) / (SIDE * SIDE)
    return (
        np.cos(angle).astype(np.float32),
        np.sin(angle).astype(np.float32),
        radius.astype(np.float32),
    )


COSINE, SINE, RADIUS = _tables()


def split3(values):
    first = values.astype(jnp.bfloat16)
    rest = values - first.astype(jnp.float32)
    second = rest.astype(jnp.bfloat16)
    third = (rest - second.astype(jnp.float32)).astype(jnp.bfloat16)
    return first, second, third


def exchange(values, axis, size):
    spread = jnp.broadcast_to(values[None], (size,) + values.shape)
    return lax.all_to_all(spread, axis, 0, 0, tiled=True)


def shards(images, defocus, inv_noise, slices, lists, counts):
    rows = images.shape[0]
    own_orients = slices.shape[0]
    orient_total = own_orients * lax.axis_size("zz") * lax.axis_size("cc")
    pad = (-(orient_total + 2)) % 128
    zz = lax.axis_index("zz")
    cc = lax.axis_index("cc")

    orient_ids = jnp.arange(orient_total, dtype=jnp.int32)
    slot_live = jnp.arange(lists.shape[1], dtype=jnp.int32)[None, :] < counts[:, None]
    hits = (lists[:, :, None] == orient_ids[None, None, :]) & slot_live[:, :, None]
    mask_all = jnp.any(hits, axis=1)
    alive = counts > 0
    extra = jnp.concatenate(
        (
            mask_all.astype(jnp.bfloat16),
            alive.astype(jnp.bfloat16)[:, None],
            defocus[:, None],
            jnp.zeros((rows, pad), jnp.bfloat16),
        ),
        axis=1,
    )
    group = lax.axis_size("zz")
    meta = exchange(extra, "zz", group).reshape(group * rows, extra.shape[1])
    g_images = lax.all_gather(images, "zz", axis=0, tiled=True)
    local_slices = lax.all_gather(slices, "cc", axis=0, tiled=True)
    count = g_images.shape[0]
    chip_orients = local_slices.shape[0]

    g_mask_all = meta[:, :orient_total]
    g_alive = meta[:, orient_total] > 0.5
    g_defocus = meta[:, orient_total + 1].astype(jnp.float32)
    mask = lax.dynamic_slice_in_dim(g_mask_all, zz * chip_orients, chip_orients, 1) > 0.5

    cosine = jnp.asarray(COSINE)
    sine = jnp.asarray(SINE)
    radius = jnp.asarray(RADIUS)
    ctf = -jnp.sin(jnp.pi * g_defocus[:, None] * radius[None, :] + 0.1)
    quad_half = (-0.5 * inv_noise * ctf * ctf).astype(jnp.bfloat16)
    ctf_half = (ctf * ctf).astype(jnp.bfloat16)
    noise_ctf = inv_noise * ctf
    ctf, noise_ctf, quad_half, ctf_half = lax.optimization_barrier((ctf, noise_ctf, quad_half, ctf_half))
    real_part = g_images[:, :COEF].astype(jnp.float32)
    imag_part = g_images[:, COEF:].astype(jnp.float32)
    weighted_r = (noise_ctf * real_part).astype(jnp.bfloat16)
    weighted_i = (noise_ctf * imag_part).astype(jnp.bfloat16)
    image_r = (ctf * real_part).astype(jnp.bfloat16)
    image_i = (ctf * imag_part).astype(jnp.bfloat16)

    slices_wide = local_slices.astype(jnp.float32)
    squares = (slices_wide * slices_wide).astype(jnp.bfloat16)
    energy = lax.dot_general(
        quad_half, squares[:, :COEF], (((1,), (1,)), ((), ())), preferred_element_type=jnp.float32
    ) + lax.dot_general(
        quad_half, squares[:, COEF:], (((1,), (1,)), ((), ())), preferred_element_type=jnp.float32
    )

    s_real = slices_wide[None, :, :COEF]
    s_imag = slices_wide[None, :, COEF:]
    c_t = cosine[:, None, :]
    s_t = sine[:, None, :]
    block = TRANS * chip_orients
    turned_r = (c_t * s_real + s_t * s_imag).reshape(block, COEF)
    turned_i = (c_t * s_imag - s_t * s_real).reshape(block, COEF)
    parts_r = jnp.concatenate(split3(turned_r), axis=0)
    parts_i = jnp.concatenate(split3(turned_i), axis=0)
    linear3 = lax.dot_general(
        weighted_r, parts_r, (((1,), (1,)), ((), ())), preferred_element_type=jnp.float32
    ) + lax.dot_general(
        weighted_i, parts_i, (((1,), (1,)), ((), ())), preferred_element_type=jnp.float32
    )
    linear = linear3[:, :block] + linear3[:, block : 2 * block] + linear3[:, 2 * block :]
    linear = linear.reshape(count, TRANS, chip_orients)
    score = jnp.where(mask[:, None, :], linear + energy[:, None, :], SENTINEL)

    local_max = jnp.max(score, axis=(1, 2))
    local_sum = jnp.sum(
        jnp.where(mask[:, None, :], jnp.exp(score - local_max[:, None, None]), 0.0), axis=(1, 2)
    )
    stats = exchange(jnp.stack((local_max, local_sum)), "zz", group)
    highest = jnp.max(stats[:, 0], axis=0)
    normalizer = jnp.sum(stats[:, 1] * jnp.exp(stats[:, 0] - highest[None, :]), axis=0)
    highest = jnp.where(g_alive, highest, 0.0)
    normalizer = jnp.where(g_alive, normalizer, 1.0)
    expo = jnp.where(mask[:, None, :], jnp.exp(score - highest[:, None, None]), 0.0)
    posterior = (expo / normalizer[:, None, None]).astype(jnp.bfloat16)
    posterior = jnp.where(g_alive[:, None, None], posterior, jnp.zeros_like(posterior))
    peak_all = jnp.where(g_alive, 1.0 / normalizer, 0.0)
    peak_weight = lax.dynamic_slice_in_dim(peak_all, zz * rows, rows, 0)

    flat_post = posterior.reshape(count, block)
    accum = lax.dot_general(
        flat_post,
        jnp.concatenate((image_r, image_i, ctf_half), axis=1),
        (((0,), (0,)), ((), ())),
        preferred_element_type=jnp.float32,
    ).reshape(TRANS, chip_orients, PIX + COEF)
    weight = jnp.sum(accum[:, :, PIX:], axis=0)
    a_real = accum[:, :, :COEF]
    a_imag = accum[:, :, COEF:PIX]
    data_real = jnp.sum(c_t * a_real - s_t * a_imag, axis=0)
    data_imag = jnp.sum(s_t * a_real + c_t * a_imag, axis=0)
    data = jnp.concatenate((data_real, data_imag), axis=-1)


    doms = lax.axis_size("dom")
    halves = lax.axis_size("cc")
    data_cols = PIX // doms
    weight_cols = COEF // doms
    data_b = data.reshape(halves, own_orients, doms, data_cols).transpose(0, 2, 1, 3)
    weight_b = weight.reshape(halves, own_orients, doms, weight_cols).transpose(0, 2, 1, 3)
    both = jnp.concatenate((data_b, weight_b), axis=-1).reshape(
        halves * doms * own_orients, data_cols + weight_cols
    )
    both = both.reshape(halves, doms, own_orients, data_cols + weight_cols)
    mine = lax.dynamic_index_in_dim(both, cc, 0, keepdims=False)
    other = lax.dynamic_index_in_dim(both, 1 - cc, 0, keepdims=False)
    paired = mine + lax.ppermute(other, "cc", [(0, 1), (1, 0)])
    moved = lax.all_to_all(paired, "dom", 0, 0, tiled=True)
    data_out = jnp.sum(moved[:, :, :data_cols], axis=0)
    weight_out = jnp.sum(moved[:, :, data_cols:], axis=0)
    return (peak_weight, data_out, weight_out)


def solution(mesh):
    doms = mesh.shape["dom"]
    slabs = mesh.shape["slab"]
    split = Mesh(mesh.devices.reshape(doms, slabs // 2, 2), ("dom", "zz", "cc"))
    rowwise = ("dom", "zz", "cc")
    placed = (
        P(rowwise, None),
        P(rowwise),
        P(),
        P(("zz", "cc"), None),
        P(rowwise, None),
        P(rowwise),
    )
    return jax.shard_map(
        shards,
        mesh=split,
        in_specs=placed,
        out_specs=(P(rowwise), P(("zz", "cc"), "dom"), P(("zz", "cc"), "dom")),
        check_vma=False,
    )
```

```python
import math

import numpy as np
import jax
import jax.numpy as jnp
from jax import lax
from jax.sharding import Mesh
from jax.sharding import PartitionSpec as P

SIDE = 64
COEF = 4096
PIX = 2 * COEF
TRANS = 25

SENTINEL = -1e30
HIGHEST = lax.Precision.HIGHEST


def _tables():
    position = np.arange(COEF)
    freq_x = (position // SIDE - SIDE // 2).astype(np.float64)
    freq_y = (position % SIDE - SIDE // 2).astype(np.float64)
    edge = math.isqrt(TRANS)
    half = edge // 2
    offsets = np.arange(TRANS)
    shift_x = (offsets // edge - half).astype(np.float64)
    shift_y = (offsets % edge - half).astype(np.float64)
    angle = 2.0 * np.pi * (shift_x[:, None] * freq_x[None, :] + shift_y[:, None] * freq_y[None, :]) / SIDE
    radius = (freq_x * freq_x + freq_y * freq_y) / (SIDE * SIDE)
    return (
        np.cos(angle).astype(np.float32),
        np.sin(angle).astype(np.float32),
        radius.astype(np.float32),
    )


COSINE, SINE, RADIUS = _tables()


def split3(values):
    first = values.astype(jnp.bfloat16)
    rest = values - first.astype(jnp.float32)
    second = rest.astype(jnp.bfloat16)
    third = (rest - second.astype(jnp.float32)).astype(jnp.bfloat16)
    return first, second, third


def exchange(values, axis, size):
    spread = jnp.broadcast_to(values[None], (size,) + values.shape)
    return lax.all_to_all(spread, axis, 0, 0, tiled=True)


def shards(images, defocus, inv_noise, slices, lists, counts):
    rows = images.shape[0]
    own_orients = slices.shape[0]
    orient_total = own_orients * lax.axis_size("zz") * lax.axis_size("cc")
    pad = (-(orient_total + 2)) % 128
    zz = lax.axis_index("zz")
    cc = lax.axis_index("cc")

    orient_ids = jnp.arange(orient_total, dtype=jnp.int32)
    slot_live = jnp.arange(lists.shape[1], dtype=jnp.int32)[None, :] < counts[:, None]
    hits = (lists[:, :, None] == orient_ids[None, None, :]) & slot_live[:, :, None]
    mask_all = jnp.any(hits, axis=1)
    alive = counts > 0
    extra = jnp.concatenate(
        (
            mask_all.astype(jnp.bfloat16),
            alive.astype(jnp.bfloat16)[:, None],
            defocus[:, None],
            jnp.zeros((rows, pad), jnp.bfloat16),
        ),
        axis=1,
    )
    group = lax.axis_size("zz")
    meta = exchange(extra, "zz", group).reshape(group * rows, extra.shape[1])
    g_images = lax.all_gather(images, "zz", axis=0, tiled=True)
    local_slices = lax.all_gather(slices, "cc", axis=0, tiled=True)
    count = g_images.shape[0]
    chip_orients = local_slices.shape[0]

    g_mask_all = meta[:, :orient_total]
    g_alive = meta[:, orient_total] > 0.5
    g_defocus = meta[:, orient_total + 1].astype(jnp.float32)
    mask = lax.dynamic_slice_in_dim(g_mask_all, zz * chip_orients, chip_orients, 1) > 0.5

    cosine = jnp.asarray(COSINE)
    sine = jnp.asarray(SINE)
    radius = jnp.asarray(RADIUS)
    ctf = -jnp.sin(jnp.pi * g_defocus[:, None] * radius[None, :] + 0.1)
    quad_half = (-0.5 * inv_noise * ctf * ctf).astype(jnp.bfloat16)
    ctf_half = (ctf * ctf).astype(jnp.bfloat16)
    noise_ctf = inv_noise * ctf
    ctf, noise_ctf, quad_half, ctf_half = lax.optimization_barrier((ctf, noise_ctf, quad_half, ctf_half))
    real_part = g_images[:, :COEF].astype(jnp.float32)
    imag_part = g_images[:, COEF:].astype(jnp.float32)
    weighted_r = (noise_ctf * real_part).astype(jnp.bfloat16)
    weighted_i = (noise_ctf * imag_part).astype(jnp.bfloat16)
    weighted_r, weighted_i = lax.optimization_barrier((weighted_r, weighted_i))
    image_r = (ctf * real_part).astype(jnp.bfloat16)
    image_i = (ctf * imag_part).astype(jnp.bfloat16)

    slices_wide = local_slices.astype(jnp.float32)
    squares = (slices_wide * slices_wide).astype(jnp.bfloat16)
    energy = lax.dot_general(
        quad_half, squares[:, :COEF], (((1,), (1,)), ((), ())), preferred_element_type=jnp.float32
    ) + lax.dot_general(
        quad_half, squares[:, COEF:], (((1,), (1,)), ((), ())), preferred_element_type=jnp.float32
    )

    s_real = slices_wide[None, :, :COEF]
    s_imag = slices_wide[None, :, COEF:]
    c_t = cosine[:, None, :]
    s_t = sine[:, None, :]
    block = TRANS * chip_orients
    turned_r = (c_t * s_real + s_t * s_imag).reshape(block, COEF)
    turned_i = (c_t * s_imag - s_t * s_real).reshape(block, COEF)
    parts_r = jnp.concatenate(split3(turned_r), axis=0)
    parts_i = jnp.concatenate(split3(turned_i), axis=0)
    linear3 = lax.dot_general(
        weighted_r, parts_r, (((1,), (1,)), ((), ())), preferred_element_type=jnp.float32
    ) + lax.dot_general(
        weighted_i, parts_i, (((1,), (1,)), ((), ())), preferred_element_type=jnp.float32
    )
    linear = linear3[:, :block] + linear3[:, block : 2 * block] + linear3[:, 2 * block :]
    linear = linear.reshape(count, TRANS, chip_orients)
    score = jnp.where(mask[:, None, :], linear + energy[:, None, :], SENTINEL)

    local_max = jnp.max(score, axis=(1, 2))
    local_sum = jnp.sum(
        jnp.where(mask[:, None, :], jnp.exp(score - local_max[:, None, None]), 0.0), axis=(1, 2)
    )
    stats = exchange(jnp.stack((local_max, local_sum)), "zz", group)
    highest = jnp.max(stats[:, 0], axis=0)
    normalizer = jnp.sum(stats[:, 1] * jnp.exp(stats[:, 0] - highest[None, :]), axis=0)
    highest = jnp.where(g_alive, highest, 0.0)
    normalizer = jnp.where(g_alive, normalizer, 1.0)
    expo = jnp.where(mask[:, None, :], jnp.exp(score - highest[:, None, None]), 0.0)
    posterior = (expo / normalizer[:, None, None]).astype(jnp.bfloat16)
    posterior = jnp.where(g_alive[:, None, None], posterior, jnp.zeros_like(posterior))
    peak_all = jnp.where(g_alive, 1.0 / normalizer, 0.0)
    peak_weight = lax.dynamic_slice_in_dim(peak_all, zz * rows, rows, 0)

    flat_post = posterior.reshape(count, block)
    accum = lax.dot_general(
        flat_post,
        jnp.concatenate((image_r, image_i, ctf_half), axis=1),
        (((0,), (0,)), ((), ())),
        preferred_element_type=jnp.float32,
    ).reshape(TRANS, chip_orients, PIX + COEF)
    weight = jnp.sum(accum[:, :, PIX:], axis=0)
    a_real = accum[:, :, :COEF]
    a_imag = accum[:, :, COEF:PIX]
    data_real = jnp.sum(c_t * a_real - s_t * a_imag, axis=0)
    data_imag = jnp.sum(s_t * a_real + c_t * a_imag, axis=0)
    data = jnp.concatenate((data_real, data_imag), axis=-1)


    doms = lax.axis_size("dom")
    halves = lax.axis_size("cc")
    data_cols = PIX // doms
    weight_cols = COEF // doms
    data_b = data.reshape(halves, own_orients, doms, data_cols).transpose(0, 2, 1, 3)
    weight_b = weight.reshape(halves, own_orients, doms, weight_cols).transpose(0, 2, 1, 3)
    both = jnp.concatenate((data_b, weight_b), axis=-1).reshape(
        halves * doms * own_orients, data_cols + weight_cols
    )
    both = both.reshape(halves, doms, own_orients, data_cols + weight_cols)
    mine = lax.dynamic_index_in_dim(both, cc, 0, keepdims=False)
    other = lax.dynamic_index_in_dim(both, 1 - cc, 0, keepdims=False)
    paired = mine + lax.ppermute(other, "cc", [(0, 1), (1, 0)])
    reduced = jnp.sum(lax.all_to_all(paired, "dom", 0, 0, tiled=True), axis=0)
    data_out = reduced[:, :data_cols]
    weight_out = reduced[:, data_cols:]
    return (peak_weight, data_out, weight_out)


def solution(mesh):
    doms = mesh.shape["dom"]
    slabs = mesh.shape["slab"]
    split = Mesh(mesh.devices.reshape(doms, slabs // 2, 2), ("dom", "zz", "cc"))
    rowwise = ("dom", "zz", "cc")
    placed = (
        P(rowwise, None),
        P(rowwise),
        P(),
        P(("zz", "cc"), None),
        P(rowwise, None),
        P(rowwise),
    )
    return jax.shard_map(
        shards,
        mesh=split,
        in_specs=placed,
        out_specs=(P(rowwise), P(("zz", "cc"), "dom"), P(("zz", "cc"), "dom")),
        check_vma=False,
    )
```

```python
import math

import numpy as np
import jax
import jax.numpy as jnp
from jax import lax
from jax.sharding import Mesh
from jax.sharding import PartitionSpec as P

SIDE = 64
COEF = 4096
PIX = 2 * COEF
TRANS = 25

SENTINEL = -1e30
HIGHEST = lax.Precision.HIGHEST


def _tables():
    position = np.arange(COEF)
    freq_x = (position // SIDE - SIDE // 2).astype(np.float64)
    freq_y = (position % SIDE - SIDE // 2).astype(np.float64)
    edge = math.isqrt(TRANS)
    half = edge // 2
    offsets = np.arange(TRANS)
    shift_x = (offsets // edge - half).astype(np.float64)
    shift_y = (offsets % edge - half).astype(np.float64)
    angle = 2.0 * np.pi * (shift_x[:, None] * freq_x[None, :] + shift_y[:, None] * freq_y[None, :]) / SIDE
    radius = (freq_x * freq_x + freq_y * freq_y) / (SIDE * SIDE)
    return (
        np.cos(angle).astype(np.float32),
        np.sin(angle).astype(np.float32),
        radius.astype(np.float32),
    )


COSINE, SINE, RADIUS = _tables()


def split3(values):
    first = values.astype(jnp.bfloat16)
    rest = values - first.astype(jnp.float32)
    second = rest.astype(jnp.bfloat16)
    third = (rest - second.astype(jnp.float32)).astype(jnp.bfloat16)
    return first, second, third


def exchange(values, axis, size):
    spread = jnp.broadcast_to(values[None], (size,) + values.shape)
    return lax.all_to_all(spread, axis, 0, 0, tiled=True)


def shards(images, defocus, inv_noise, slices, lists, counts):
    rows = images.shape[0]
    own_orients = slices.shape[0]
    orient_total = own_orients * lax.axis_size("zz") * lax.axis_size("cc")
    pad = (-(orient_total + 2)) % 128
    zz = lax.axis_index("zz")
    cc = lax.axis_index("cc")

    orient_ids = jnp.arange(orient_total, dtype=jnp.int32)
    slot_live = jnp.arange(lists.shape[1], dtype=jnp.int32)[None, :] < counts[:, None]
    hits = (lists[:, :, None] == orient_ids[None, None, :]) & slot_live[:, :, None]
    mask_all = jnp.any(hits, axis=1)
    alive = counts > 0
    extra = jnp.concatenate(
        (
            mask_all.astype(jnp.bfloat16),
            alive.astype(jnp.bfloat16)[:, None],
            defocus[:, None],
            jnp.zeros((rows, pad), jnp.bfloat16),
        ),
        axis=1,
    )
    group = lax.axis_size("zz")
    meta = exchange(extra, "zz", group).reshape(group * rows, extra.shape[1])
    g_images = lax.all_gather(images, "zz", axis=0, tiled=True)
    local_slices = lax.all_gather(slices, "cc", axis=0, tiled=True)
    count = g_images.shape[0]
    chip_orients = local_slices.shape[0]

    g_mask_all = meta[:, :orient_total]
    g_alive = meta[:, orient_total] > 0.5
    g_defocus = meta[:, orient_total + 1].astype(jnp.float32)
    mask = lax.dynamic_slice_in_dim(g_mask_all, zz * chip_orients, chip_orients, 1) > 0.5

    cosine = jnp.asarray(COSINE)
    sine = jnp.asarray(SINE)
    radius = jnp.asarray(RADIUS)
    ctf = -jnp.sin(jnp.pi * g_defocus[:, None] * radius[None, :] + 0.1)
    quad_half = (-0.5 * inv_noise * ctf * ctf).astype(jnp.bfloat16)
    ctf_half = (ctf * ctf).astype(jnp.bfloat16)
    noise_ctf = inv_noise * ctf
    ctf, noise_ctf, quad_half, ctf_half = lax.optimization_barrier((ctf, noise_ctf, quad_half, ctf_half))
    real_part = g_images[:, :COEF].astype(jnp.float32)
    imag_part = g_images[:, COEF:].astype(jnp.float32)
    weighted_r = (noise_ctf * real_part).astype(jnp.bfloat16)
    weighted_i = (noise_ctf * imag_part).astype(jnp.bfloat16)
    image_r = (ctf * real_part).astype(jnp.bfloat16)
    image_i = (ctf * imag_part).astype(jnp.bfloat16)

    slices_wide = local_slices.astype(jnp.float32)
    squares = (slices_wide * slices_wide).astype(jnp.bfloat16)
    energy = lax.dot_general(
        quad_half, squares[:, :COEF], (((1,), (1,)), ((), ())), preferred_element_type=jnp.float32
    ) + lax.dot_general(
        quad_half, squares[:, COEF:], (((1,), (1,)), ((), ())), preferred_element_type=jnp.float32
    )

    s_real = slices_wide[None, :, :COEF]
    s_imag = slices_wide[None, :, COEF:]
    c_t = cosine[:, None, :]
    s_t = sine[:, None, :]
    block = TRANS * chip_orients
    turned_r = (c_t * s_real + s_t * s_imag).reshape(block, COEF)
    turned_i = (c_t * s_imag - s_t * s_real).reshape(block, COEF)
    parts_r = jnp.concatenate(split3(turned_r), axis=0)
    parts_i = jnp.concatenate(split3(turned_i), axis=0)
    linear3 = lax.dot_general(
        weighted_i, parts_i, (((1,), (1,)), ((), ())), preferred_element_type=jnp.float32
    ) + lax.dot_general(
        weighted_r, parts_r, (((1,), (1,)), ((), ())), preferred_element_type=jnp.float32
    )
    linear = linear3[:, :block] + linear3[:, block : 2 * block] + linear3[:, 2 * block :]
    linear = linear.reshape(count, TRANS, chip_orients)
    score = jnp.where(mask[:, None, :], linear + energy[:, None, :], SENTINEL)

    local_max = jnp.max(score, axis=(1, 2))
    local_sum = jnp.sum(
        jnp.where(mask[:, None, :], jnp.exp(score - local_max[:, None, None]), 0.0), axis=(1, 2)
    )
    stats = exchange(jnp.stack((local_max, local_sum)), "zz", group)
    highest = jnp.max(stats[:, 0], axis=0)
    normalizer = jnp.sum(stats[:, 1] * jnp.exp(stats[:, 0] - highest[None, :]), axis=0)
    highest = jnp.where(g_alive, highest, 0.0)
    normalizer = jnp.where(g_alive, normalizer, 1.0)
    expo = jnp.where(mask[:, None, :], jnp.exp(score - highest[:, None, None]), 0.0)
    posterior = (expo / normalizer[:, None, None]).astype(jnp.bfloat16)
    posterior = jnp.where(g_alive[:, None, None], posterior, jnp.zeros_like(posterior))
    peak_all = jnp.where(g_alive, 1.0 / normalizer, 0.0)
    peak_weight = lax.dynamic_slice_in_dim(peak_all, zz * rows, rows, 0)

    flat_post = posterior.reshape(count, block)
    accum = lax.dot_general(
        flat_post,
        jnp.concatenate((image_r, image_i), axis=1),
        (((0,), (0,)), ((), ())),
        preferred_element_type=jnp.float32,
    ).reshape(TRANS, chip_orients, PIX)
    per_orient = jnp.sum(posterior.astype(jnp.float32), axis=1)
    weight3 = lax.dot_general(
        jnp.concatenate(split3(per_orient), axis=1),
        ctf_half,
        (((0,), (0,)), ((), ())),
        preferred_element_type=jnp.float32,
    )
    weight = (
        weight3[:chip_orients] + weight3[chip_orients : 2 * chip_orients] + weight3[2 * chip_orients :]
    )
    a_real = accum[:, :, :COEF]
    a_imag = accum[:, :, COEF:PIX]
    data_real = jnp.sum(c_t * a_real - s_t * a_imag, axis=0)
    data_imag = jnp.sum(s_t * a_real + c_t * a_imag, axis=0)
    data = jnp.concatenate((data_real, data_imag), axis=-1)


    doms = lax.axis_size("dom")
    halves = lax.axis_size("cc")
    data_cols = PIX // doms
    weight_cols = COEF // doms
    data_b = data.reshape(halves, own_orients, doms, data_cols).transpose(0, 2, 1, 3)
    weight_b = weight.reshape(halves, own_orients, doms, weight_cols).transpose(0, 2, 1, 3)
    both = jnp.concatenate((data_b, weight_b), axis=-1).reshape(
        halves * doms * own_orients, data_cols + weight_cols
    )
    both = both.reshape(halves, doms, own_orients, data_cols + weight_cols)
    mine = lax.dynamic_index_in_dim(both, cc, 0, keepdims=False)
    other = lax.dynamic_index_in_dim(both, 1 - cc, 0, keepdims=False)
    paired = mine + lax.ppermute(other, "cc", [(0, 1), (1, 0)])
    reduced = jnp.sum(lax.all_to_all(paired, "dom", 0, 0, tiled=True), axis=0)
    data_out = reduced[:, :data_cols]
    weight_out = reduced[:, data_cols:]
    return (peak_weight, data_out, weight_out)


def solution(mesh):
    doms = mesh.shape["dom"]
    slabs = mesh.shape["slab"]
    split = Mesh(mesh.devices.reshape(doms, slabs // 2, 2), ("dom", "zz", "cc"))
    rowwise = ("dom", "zz", "cc")
    placed = (
        P(rowwise, None),
        P(rowwise),
        P(),
        P(("zz", "cc"), None),
        P(rowwise, None),
        P(rowwise),
    )
    return jax.shard_map(
        shards,
        mesh=split,
        in_specs=placed,
        out_specs=(P(rowwise), P(("zz", "cc"), "dom"), P(("zz", "cc"), "dom")),
        check_vma=False,
    )
```
